32 devices in a mesh: row: 8 (over y, x, core), col: 4 (over z).
Axes of the slice: x: 2, y: 2, z: 4, core: 2. Of those that a mesh axis runs over, the one named last changes fastest.
Arguments:
- a_blocks: bfloat16 [8, 4, 16, 128, 128], P('row', 'col'), may hold values from -6 to 6
- b_blocks: bfloat16 [8, 4, 16, 128, 128], P('row', 'col'), may hold values from -0.21875 to 0.21875
- a_send: int32 [8, 4, 4, 4], P('row', 'col'), may hold values from -1 to 15, as said below
- b_send: int32 [8, 4, 8, 2], P('row', 'col'), may hold values from -1 to 15, as said below
- triples: int32 [8, 4, 4, 3, 384], P('row', 'col'), may hold values from -1 to 15, as said below
- c_send: int32 [8, 4, 32], P('row', 'col'), may hold values from -1 to 15, as said below
Outputs:
- returned: bfloat16 [8, 4, 32, 128, 128], P('row', 'col')
The draws below stay inside these ranges and needn't reach their ends.
Inputs may be any that keep to these rules, and one draw needn't show every extreme that they name: In a_send[r, j], every block 0 to 15 appears exactly once; in every grid row one owner column receives 4 blocks from every column, which one is drawn. In b_send[i, c], every block 0 to 15 appears exactly once; in every grid column one owner row receives 2 blocks from every row, which one is drawn. Left slots are below 16, right slots below 16, result blocks below 16; live triples name panel slots that hold a stored block wherever the panel meeting there holds any; in each stack the live triples come first, or all three entries are -1; each stack holds 192 to 384 live triples, and at every stop some device holds 384. `c_send`: each device returns each of its 16 result blocks to exactly one device; one drawn device receives a block from every device.
All inputs are finite; a program needn't handle non-finite values.
Results may differ from the reference program's by a relative error of at most 0.0049.
Values may be sent and summed in bfloat16 or wider, within the bound.
No kernel may reach another device: no remote copies, remote signals or barrier semaphores. Data moves between devices by JAX's collectives and lax.ppermute only.
A program may use at most 64 MiB of HBM per device.

```python
import jax
import jax.numpy as jnp
from jax import lax

BS = 128
PA = 16
CAP_A = 4
PB = 16
CAP_B = 2
NS = 384
STOPS = 4
LOOP_R = 8
LOOP_C = 4
SA = 16
SB = 16
NC = 16


def spread_list(key, blocks, dests, cap, center):
    first_key = jax.random.fold_in(key, 1)
    second_key = jax.random.fold_in(key, 2)
    order = jax.random.permutation(first_key, blocks).astype(jnp.int32)
    extra = jax.random.permutation(second_key, (dests - 1) * cap)[:blocks - cap].astype(jnp.int32)
    column = extra // cap
    column = column + (column >= center).astype(jnp.int32)
    place = jnp.concatenate([center * cap + jnp.arange(cap, dtype=jnp.int32), column * cap + extra % cap]).astype(jnp.int32)
    table = jnp.full((dests * cap,), -1, jnp.int32).at[place].set(order)
    return table.reshape(dests, cap)


def draw_a_send(key, part):
    centers = jax.random.randint(jax.random.fold_in(key, 11), (LOOP_R,), 0, LOOP_C)
    base = jax.random.fold_in(key, 12)
    numbers = jnp.arange(LOOP_R * LOOP_C, dtype=jnp.int32).reshape(LOOP_R, LOOP_C)

    def per_row(row_numbers, center):
        return jax.vmap(lambda number: spread_list(jax.random.fold_in(base, number), PA, LOOP_C, CAP_A, center))(row_numbers)
    return jax.vmap(per_row)(numbers, centers)


def draw_b_send(key, part):
    centers = jax.random.randint(jax.random.fold_in(key, 21), (LOOP_C,), 0, LOOP_R)
    base = jax.random.fold_in(key, 22)
    numbers = jnp.arange(LOOP_R * LOOP_C, dtype=jnp.int32).reshape(LOOP_R, LOOP_C)

    def per_row(row_numbers):
        return jax.vmap(lambda number, center: spread_list(jax.random.fold_in(base, number), PB, LOOP_R, CAP_B, center))(row_numbers, centers)
    return jax.vmap(per_row)(numbers)


def pick_live(key, mask):
    order = jnp.argsort(1 - mask.astype(jnp.int32), axis=-1, stable=True).astype(jnp.int32)
    live_count = jnp.maximum(jnp.sum(mask.astype(jnp.int32), axis=-1), 1)
    chosen = jax.random.randint(key, mask.shape[:-1] + (NS,), 0, live_count[..., None])
    return jnp.take_along_axis(order, chosen.astype(jnp.int32), axis=-1).astype(jnp.int32)


def draw_triples(key, part):
    count = LOOP_R * LOOP_C
    a_send = draw_a_send(key, part)
    b_send = draw_b_send(key, part)
    a_live = jnp.transpose(a_send, (0, 2, 1, 3)).reshape(LOOP_R, LOOP_C, SA) >= 0
    b_live = jnp.transpose(b_send, (2, 1, 0, 3)).reshape(LOOP_R, LOOP_C, SB) >= 0
    rows_at = jnp.arange(LOOP_R)[:, None, None]
    cols_at = jnp.arange(LOOP_C)[None, :, None]
    stops_at = jnp.arange(STOPS)[None, None, :]
    left_mask = a_live[rows_at, (cols_at + stops_at) % LOOP_C]
    right_mask = b_live[(rows_at + stops_at) % LOOP_R, cols_at]
    left = pick_live(jax.random.fold_in(key, 33), left_mask).reshape(count, STOPS, NS)
    right = pick_live(jax.random.fold_in(key, 34), right_mask).reshape(count, STOPS, NS)
    live = jax.random.randint(jax.random.fold_in(key, 31), (count, STOPS), NS // 2, NS + 1)
    fullest = jax.random.randint(jax.random.fold_in(key, 32), (STOPS,), 0, count)
    live = jnp.where(jnp.arange(count)[:, None] == fullest[None, :], NS, live)
    target = jax.random.randint(jax.random.fold_in(key, 35), (count, STOPS, NS), 0, NC)
    stacked = jnp.stack([left, right, target], axis=2)
    inside = jnp.arange(NS)[None, None, None, :] < live[:, :, None, None]
    stacked = jnp.where(inside, stacked, -1).astype(jnp.int32)
    return stacked.reshape(LOOP_R, LOOP_C, STOPS, 3, NS)


def draw_c_send(key, part):
    count = LOOP_R * LOOP_C
    center = jax.random.randint(jax.random.fold_in(key, 41), (), 0, count)
    base = jax.random.fold_in(key, 42)

    def per_device(number):
        single = jax.random.fold_in(base, number)
        first_key = jax.random.fold_in(single, 1)
        second_key = jax.random.fold_in(single, 2)
        others = jax.random.permutation(first_key, count - 1)[:NC - 1].astype(jnp.int32)
        others = others + (others >= center).astype(jnp.int32)
        dests = jnp.concatenate([center[None].astype(jnp.int32), others])
        slots = jax.random.permutation(second_key, NC).astype(jnp.int32)
        return jnp.full((count,), -1, jnp.int32).at[dests].set(slots)
    return jax.vmap(per_device)(jnp.arange(count, dtype=jnp.int32)).reshape(LOOP_R, LOOP_C, count)


def shard_levels(rng, dims, pieces, low, top_value):
    gain = 1.0
    for axis_at, parts in pieces:
        heights = jax.random.uniform(jax.random.fold_in(jax.random.fold_in(rng, 6), axis_at), (parts,), jnp.float32, low / len(pieces), top_value / len(pieces))
        gain = gain * jnp.repeat(jnp.exp(heights), dims[axis_at] // parts).reshape((-1,) + (1,) * (len(dims) - 1 - axis_at))
    return gain


def bell_draw(own_key, extent, deviation, limit, split=(), kind=jnp.bfloat16):
    loudness = shard_levels(own_key, extent, split, -0.22, 0.18) if split else 1.0
    values = jax.random.normal(own_key, extent, jnp.float32) * deviation * loudness
    return jnp.minimum(jnp.maximum(values, -limit), limit).astype(kind)


def setup_inputs(seed: int = 0) -> dict:
    streams_of = jax.random.split(jax.random.key(seed), 7)
    return {
        "a_blocks": bell_draw(streams_of[0], (LOOP_R, LOOP_C, PA, BS, BS), 1.0, 6.0, ((0, 8), (1, 4))),
        "b_blocks": bell_draw(streams_of[1], (LOOP_R, LOOP_C, PB, BS, BS), (6 * BS) ** -0.5, 0.21875, ((0, 8), (1, 4))),
        "a_send": draw_a_send(jax.random.fold_in(streams_of[6], 71), 0),
        "b_send": draw_b_send(jax.random.fold_in(streams_of[6], 71), 0),
        "triples": draw_triples(jax.random.fold_in(streams_of[6], 71), 0),
        "c_send": draw_c_send(jax.random.fold_in(streams_of[6], 71), 0),
    }


def reference(a_blocks, b_blocks, a_send, b_send, triples, c_send):
    rows_n = LOOP_R
    cols_n = LOOP_C
    count = rows_n * cols_n
    a_index = jnp.transpose(a_send, (0, 2, 1, 3))
    a_taken = a_blocks[jnp.arange(rows_n)[:, None, None, None], jnp.arange(cols_n)[None, None, :, None], jnp.maximum(a_index, 0)]
    a_taken = jnp.where((a_index >= 0)[..., None, None], a_taken, jnp.zeros_like(a_taken))
    a_panel = a_taken.reshape(rows_n, cols_n, SA, BS, BS)
    b_index = jnp.transpose(b_send, (2, 1, 0, 3))
    b_taken = b_blocks[jnp.arange(rows_n)[None, None, :, None], jnp.arange(cols_n)[None, :, None, None], jnp.maximum(b_index, 0)]
    b_taken = jnp.where((b_index >= 0)[..., None, None], b_taken, jnp.zeros_like(b_taken))
    b_panel = b_taken.reshape(rows_n, cols_n, SB, BS, BS)

    def one_device(number):
        grid_r = number // cols_n
        grid_c = number % cols_n
        total = jnp.zeros((NC, BS, BS), jnp.float32)
        for stop_index in range(STOPS):
            left = a_panel[grid_r, (grid_c + stop_index) % cols_n]
            right = b_panel[(grid_r + stop_index) % rows_n, grid_c]
            stack = triples[grid_r, grid_c, stop_index]
            live = (stack[0] >= 0).astype(jnp.float32)
            left_ops = left[jnp.maximum(stack[0], 0)].astype(jnp.float32)
            right_ops = right[jnp.maximum(stack[1], 0)].astype(jnp.float32)
            prods = jnp.einsum("nij,njk->nik", left_ops, right_ops, precision=lax.Precision.HIGHEST)
            prods = prods.astype(jnp.bfloat16).astype(jnp.float32)
            prods = prods * live[:, None, None]
            total = total + jax.ops.segment_sum(prods, jnp.maximum(stack[2], 0), NC)
        return total.astype(jnp.bfloat16)

    result = lax.map(one_device, jnp.arange(count, dtype=jnp.int32))
    wanted = c_send.reshape(count, count).T
    picked = result[jnp.arange(count)[None, :], jnp.maximum(wanted, 0)]
    picked = jnp.where((wanted >= 0)[..., None, None], picked, jnp.zeros_like(picked))
    return picked.reshape(rows_n, cols_n, count, BS, BS)
```

```python
import functools

import jax
import jax.numpy as jnp
from jax import lax
from jax.experimental import pallas as pl
from jax.experimental.pallas import tpu as pltpu
from jax.sharding import PartitionSpec as P

STOPS = 4


def passed_along(value, axis, steps):
    count = lax.axis_size(axis)
    pairs = [(source, (source + steps) % count) for source in range(count)]
    return lax.ppermute(value, axis, pairs)


def bucketize(blocks, index):
    picked = jnp.take(blocks, jnp.maximum(index, 0), axis=0)
    return jnp.where((index >= 0)[..., None, None], picked, jnp.zeros_like(picked))


def sort_stack(stack, left_count, right_count, result_count):
    live = stack[0] >= 0
    target = jnp.clip(stack[2], 0, result_count - 1)
    keys = jnp.where(live, target, result_count)
    order = jnp.argsort(keys, stable=True)
    left_sorted = jnp.clip(jnp.take(stack[0], order), 0, left_count - 1)
    right_sorted = jnp.clip(jnp.take(stack[1], order), 0, right_count - 1)
    counts = jnp.sum(
        (keys[:, None] == jnp.arange(result_count, dtype=jnp.int32)[None, :]).astype(jnp.int32),
        axis=0,
    )
    offsets = jnp.concatenate([jnp.zeros((1,), jnp.int32), jnp.cumsum(counts).astype(jnp.int32)])
    return left_sorted.astype(jnp.int32), right_sorted.astype(jnp.int32), offsets


def stop_kernel(ls_ref, rs_ref, off_ref, left_ref, right_ref, acc_in_ref, acc_out_ref):
    result_count = acc_out_ref.shape[0]

    def per_target(t, carry):
        def per_triple(i, acc):
            a = left_ref[ls_ref[i]]
            b = right_ref[rs_ref[i]]
            return acc + jnp.dot(a, b, preferred_element_type=jnp.float32)

        acc = lax.fori_loop(off_ref[t], off_ref[t + 1], per_triple, acc_in_ref[t])
        acc_out_ref[t] = acc
        return carry

    lax.fori_loop(0, result_count, per_target, 0)


def run_stop(total, left, right, stack):
    result_count = total.shape[0]
    ls, rs, off = sort_stack(stack, left.shape[0], right.shape[0], result_count)
    full = lambda shape: pl.BlockSpec(shape, lambda *_: (0,) * len(shape))
    grid_spec = pltpu.PrefetchScalarGridSpec(
        num_scalar_prefetch=3,
        grid=(1,),
        in_specs=[full(left.shape), full(right.shape), full(total.shape)],
        out_specs=full(total.shape),
    )
    return pl.pallas_call(
        stop_kernel,
        grid_spec=grid_spec,
        out_shape=jax.ShapeDtypeStruct(total.shape, jnp.float32),
        input_output_aliases={5: 0},
    )(ls, rs, off, left, right, total)


def on_device(a_blocks, b_blocks, a_send, b_send, triples, c_send):
    rows_n = lax.axis_size("row")
    cols_n = lax.axis_size("col")
    count = rows_n * cols_n
    result_count = count // 2
    edge = a_blocks.shape[-1]
    left_out = bucketize(a_blocks[0, 0], a_send[0, 0])
    left_home = lax.all_to_all(left_out, "col", split_axis=0, concat_axis=0, tiled=True)
    left_home = left_home.reshape(-1, edge, edge)
    right_out = bucketize(b_blocks[0, 0], b_send[0, 0])
    right_home = lax.all_to_all(right_out, "row", split_axis=0, concat_axis=0, tiled=True)
    right_home = right_home.reshape(-1, edge, edge)
    total = jnp.zeros((result_count, edge, edge), jnp.float32)
    left_now = left_home
    right_now = right_home
    for stop_index in range(STOPS):
        if stop_index > 0:
            left_now = passed_along(left_now, "col", -1)
            right_now = passed_along(right_now, "row", -1)
        total = run_stop(total, left_now, right_now, triples[0, 0, stop_index])
    result = total.astype(jnp.bfloat16)
    outgoing = bucketize(result, c_send[0, 0])
    arrived = lax.all_to_all(outgoing, ("row", "col"), split_axis=0, concat_axis=0, tiled=True)
    return arrived[None, None]


def solution(mesh):
    placed = (
        P("row", "col", None, None, None),
        P("row", "col", None, None, None),
        P("row", "col", None, None),
        P("row", "col", None, None),
        P("row", "col", None, None, None),
        P("row", "col", None),
    )
    return jax.shard_map(
        on_device,
        mesh=mesh,
        in_specs=placed,
        out_specs=P("row", "col", None, None, None),
        check_vma=False,
    )
```

```python
import functools

import jax
import jax.numpy as jnp
from jax import lax
from jax.experimental import pallas as pl
from jax.experimental.pallas import tpu as pltpu
from jax.sharding import PartitionSpec as P

STOPS = 4


def passed_along(value, axis, steps):
    count = lax.axis_size(axis)
    pairs = [(source, (source + steps) % count) for source in range(count)]
    return lax.ppermute(value, axis, pairs)


def bucketize(blocks, index):
    picked = jnp.take(blocks, jnp.maximum(index, 0), axis=0)
    return jnp.where((index >= 0)[..., None, None], picked, jnp.zeros_like(picked))


GROUP = 32


def stop_kernel(ls_ref, rs_ref, ts_ref, n_ref, left_ref, right_ref, acc_in_ref, acc_out_ref):
    live_count = n_ref[0]

    def per_group(g, carry):
        base = g * GROUP
        prods = []
        for k in range(GROUP):
            i = base + k
            p = jnp.dot(left_ref[ls_ref[i]], right_ref[rs_ref[i]], preferred_element_type=jnp.float32)
            p = p.astype(jnp.bfloat16).astype(jnp.float32)
            prods.append(jnp.where(i < live_count, p, 0.0))
        for k in range(GROUP):
            t = ts_ref[base + k]
            acc_out_ref[t] = acc_out_ref[t] + prods[k]
        return carry

    acc_out_ref[...] = acc_in_ref[...]
    lax.fori_loop(0, (live_count + GROUP - 1) // GROUP, per_group, 0)


def run_stop(total, left, right, stack):
    result_count = total.shape[0]
    slots = stack.shape[1]
    assert slots % GROUP == 0
    ls = jnp.clip(stack[0], 0, left.shape[0] - 1).astype(jnp.int32)
    rs = jnp.clip(stack[1], 0, right.shape[0] - 1).astype(jnp.int32)
    ts = jnp.clip(stack[2], 0, result_count - 1).astype(jnp.int32)
    live_count = jnp.sum((stack[0] >= 0).astype(jnp.int32)).reshape(1)
    full = lambda shape: pl.BlockSpec(shape, lambda *_: (0,) * len(shape))
    grid_spec = pltpu.PrefetchScalarGridSpec(
        num_scalar_prefetch=4,
        grid=(1,),
        in_specs=[full(left.shape), full(right.shape), full(total.shape)],
        out_specs=full(total.shape),
    )
    return pl.pallas_call(
        stop_kernel,
        grid_spec=grid_spec,
        out_shape=jax.ShapeDtypeStruct(total.shape, jnp.float32),
        input_output_aliases={6: 0},
    )(ls, rs, ts, live_count, left, right, total)


def on_device(a_blocks, b_blocks, a_send, b_send, triples, c_send):
    rows_n = lax.axis_size("row")
    cols_n = lax.axis_size("col")
    count = rows_n * cols_n
    result_count = count // 2
    edge = a_blocks.shape[-1]
    left_out = bucketize(a_blocks[0, 0], a_send[0, 0])
    left_home = lax.all_to_all(left_out, "col", split_axis=0, concat_axis=0, tiled=True)
    left_home = left_home.reshape(-1, edge, edge)
    right_out = bucketize(b_blocks[0, 0], b_send[0, 0])
    right_home = lax.all_to_all(right_out, "row", split_axis=0, concat_axis=0, tiled=True)
    right_home = right_home.reshape(-1, edge, edge)
    total = jnp.zeros((result_count, edge, edge), jnp.float32)
    left_now = left_home
    right_now = right_home
    for stop_index in range(STOPS):
        if stop_index > 0:
            left_now = passed_along(left_now, "col", -1)
            right_now = passed_along(right_now, "row", -1)
        total = run_stop(total, left_now, right_now, triples[0, 0, stop_index])
    result = total.astype(jnp.bfloat16)
    outgoing = bucketize(result, c_send[0, 0])
    arrived = lax.all_to_all(outgoing, ("row", "col"), split_axis=0, concat_axis=0, tiled=True)
    return arrived[None, None]


def solution(mesh):
    placed = (
        P("row", "col", None, None, None),
        P("row", "col", None, None, None),
        P("row", "col", None, None),
        P("row", "col", None, None),
        P("row", "col", None, None, None),
        P("row", "col", None),
    )
    return jax.shard_map(
        on_device,
        mesh=mesh,
        in_specs=placed,
        out_specs=P("row", "col", None, None, None),
        check_vma=False,
    )
```

```python
import functools

import jax
import jax.numpy as jnp
from jax import lax
from jax.experimental import pallas as pl
from jax.experimental.pallas import tpu as pltpu
from jax.sharding import PartitionSpec as P

STOPS = 4


def passed_along(value, axis, steps):
    count = lax.axis_size(axis)
    pairs = [(source, (source + steps) % count) for source in range(count)]
    return lax.ppermute(value, axis, pairs)


def bucketize(blocks, index):
    picked = jnp.take(blocks, jnp.maximum(index, 0), axis=0)
    return jnp.where((index >= 0)[..., None, None], picked, jnp.zeros_like(picked))


GROUP = 32


def stop_kernel(ls_ref, rs_ref, ts_ref, n_ref, left_ref, right_ref, acc_in_ref, acc_out_ref):
    live_count = n_ref[0]

    def per_group(g, carry):
        base = g * GROUP
        prods = []
        for k in range(GROUP):
            i = base + k
            p = jnp.dot(left_ref[ls_ref[i]], right_ref[rs_ref[i]], preferred_element_type=jnp.float32)
            p = p.astype(jnp.bfloat16).astype(jnp.float32)
            prods.append(jnp.where(i < live_count, p, 0.0))
        for k in range(GROUP):
            t = ts_ref[base + k]
            acc_out_ref[t] = acc_out_ref[t] + prods[k]
        return carry

    acc_out_ref[...] = acc_in_ref[...]
    lax.fori_loop(0, (live_count + GROUP - 1) // GROUP, per_group, 0)


def run_stop(total, left, right, stack):
    result_count = total.shape[0]
    slots = stack.shape[1]
    assert slots % GROUP == 0
    ls = jnp.clip(stack[0], 0, left.shape[0] - 1).astype(jnp.int32)
    rs = jnp.clip(stack[1], 0, right.shape[0] - 1).astype(jnp.int32)
    ts = jnp.clip(stack[2], 0, result_count - 1).astype(jnp.int32)
    live_count = jnp.sum((stack[0] >= 0).astype(jnp.int32)).reshape(1)
    full = lambda shape: pl.BlockSpec(shape, lambda *_: (0,) * len(shape))
    grid_spec = pltpu.PrefetchScalarGridSpec(
        num_scalar_prefetch=4,
        grid=(1,),
        in_specs=[full(left.shape), full(right.shape), full(total.shape)],
        out_specs=full(total.shape),
    )
    return pl.pallas_call(
        stop_kernel,
        grid_spec=grid_spec,
        out_shape=jax.ShapeDtypeStruct(total.shape, jnp.float32),
        input_output_aliases={6: 0},
    )(ls, rs, ts, live_count, left, right, total)


def on_device(a_blocks, b_blocks, a_send, b_send, triples, c_send):
    rows_n = lax.axis_size("row")
    cols_n = lax.axis_size("col")
    count = rows_n * cols_n
    result_count = count // 2
    edge = a_blocks.shape[-1]
    left_out = bucketize(a_blocks[0, 0], a_send[0, 0])
    left_home = lax.all_to_all(left_out, "col", split_axis=0, concat_axis=0, tiled=True)
    left_home = left_home.reshape(-1, edge, edge)
    right_out = bucketize(b_blocks[0, 0], b_send[0, 0])
    right_home = lax.all_to_all(right_out, "row", split_axis=0, concat_axis=0, tiled=True)
    right_home = right_home.reshape(-1, edge, edge)
    total = jnp.zeros((result_count, edge, edge), jnp.float32)
    lefts = [left_home] + [passed_along(left_home, "col", -s) for s in range(1, STOPS)]
    rights = [right_home] + [passed_along(right_home, "row", -s) for s in range(1, STOPS)]
    for stop_index in range(STOPS):
        total = run_stop(total, lefts[stop_index], rights[stop_index], triples[0, 0, stop_index])
    result = total.astype(jnp.bfloat16)
    outgoing = bucketize(result, c_send[0, 0])
    arrived = lax.all_to_all(outgoing, ("row", "col"), split_axis=0, concat_axis=0, tiled=True)
    return arrived[None, None]


def solution(mesh):
    placed = (
        P("row", "col", None, None, None),
        P("row", "col", None, None, None),
        P("row", "col", None, None),
        P("row", "col", None, None),
        P("row", "col", None, None, None),
        P("row", "col", None),
    )
    return jax.shard_map(
        on_device,
        mesh=mesh,
        in_specs=placed,
        out_specs=P("row", "col", None, None, None),
        check_vma=False,
    )
```

```python
import functools

import jax
import jax.numpy as jnp
from jax import lax
from jax.experimental import pallas as pl
from jax.experimental.pallas import tpu as pltpu
from jax.sharding import PartitionSpec as P

STOPS = 4


def passed_along(value, axis, steps):
    count = lax.axis_size(axis)
    pairs = [(source, (source + steps) % count) for source in range(count)]
    return lax.ppermute(value, axis, pairs)


def bucketize(blocks, index):
    picked = jnp.take(blocks, jnp.maximum(index, 0), axis=0)
    return jnp.where((index >= 0)[..., None, None], picked, jnp.zeros_like(picked))


GROUP = 32


def stop_kernel(ls_ref, rs_ref, ts_ref, ok_ref, n_ref, left_ref, right_ref, acc_in_ref, acc_out_ref):
    live_count = n_ref[0]

    def per_group(g, carry):
        base = g * GROUP
        prods = []
        for k in range(GROUP):
            i = base + k
            p = jnp.dot(left_ref[ls_ref[i]], right_ref[rs_ref[i]], preferred_element_type=jnp.float32)
            p = p.astype(jnp.bfloat16).astype(jnp.float32)
            prods.append(jnp.where((i < live_count) & (ok_ref[i] > 0), p, 0.0))
        for k in range(GROUP):
            t = ts_ref[base + k]
            acc_out_ref[t] = acc_out_ref[t] + prods[k]
        return carry

    acc_out_ref[...] = acc_in_ref[...]
    lax.fori_loop(0, (live_count + GROUP - 1) // GROUP, per_group, 0)


def run_stop(total, left, right, stack, left_map):
    result_count = total.shape[0]
    slots = stack.shape[1]
    assert slots % GROUP == 0
    live = stack[0] >= 0
    mapped = jnp.take(left_map, jnp.clip(stack[0], 0, left_map.shape[0] - 1))
    ok = (live & (mapped >= 0)).astype(jnp.int32)
    ls = jnp.clip(mapped, 0, left.shape[0] - 1).astype(jnp.int32)
    rs = jnp.clip(stack[1], 0, right.shape[0] - 1).astype(jnp.int32)
    ts = jnp.clip(stack[2], 0, result_count - 1).astype(jnp.int32)
    live_count = jnp.sum(live.astype(jnp.int32)).reshape(1)
    full = lambda shape: pl.BlockSpec(shape, lambda *_: (0,) * len(shape))
    grid_spec = pltpu.PrefetchScalarGridSpec(
        num_scalar_prefetch=5,
        grid=(1,),
        in_specs=[full(left.shape), full(right.shape), full(total.shape)],
        out_specs=full(total.shape),
    )
    return pl.pallas_call(
        stop_kernel,
        grid_spec=grid_spec,
        out_shape=jax.ShapeDtypeStruct(total.shape, jnp.float32),
        input_output_aliases={7: 0},
    )(ls, rs, ts, ok, live_count, left, right, total)


def on_device(a_blocks, b_blocks, a_send, b_send, triples, c_send):
    rows_n = lax.axis_size("row")
    cols_n = lax.axis_size("col")
    count = rows_n * cols_n
    result_count = count // 2
    edge = a_blocks.shape[-1]
    held = a_blocks.shape[2]
    left_all = lax.all_gather(a_blocks[0, 0], "col", axis=0, tiled=True)
    send_all = lax.all_gather(a_send[0, 0], "col", axis=0, tiled=False)
    col_at = lax.axis_index("col")
    column_base = (jnp.arange(cols_n, dtype=jnp.int32) * held)[:, None]
    left_maps = []
    for stop_index in range(STOPS):
        owner = (col_at + stop_index) % cols_n
        picked = jnp.take(send_all, owner, axis=1)
        left_maps.append(jnp.where(picked >= 0, picked + column_base, -1).reshape(-1).astype(jnp.int32))
    right_out = bucketize(b_blocks[0, 0], b_send[0, 0])
    right_home = lax.all_to_all(right_out, "row", split_axis=0, concat_axis=0, tiled=True)
    right_home = right_home.reshape(-1, edge, edge)
    total = jnp.zeros((result_count, edge, edge), jnp.float32)
    rights = [right_home] + [passed_along(right_home, "row", -s) for s in range(1, STOPS)]
    for stop_index in range(STOPS):
        total = run_stop(total, left_all, rights[stop_index], triples[0, 0, stop_index], left_maps[stop_index])
    result = total.astype(jnp.bfloat16)
    outgoing = bucketize(result, c_send[0, 0])
    arrived = lax.all_to_all(outgoing, ("row", "col"), split_axis=0, concat_axis=0, tiled=True)
    return arrived[None, None]


def solution(mesh):
    placed = (
        P("row", "col", None, None, None),
        P("row", "col", None, None, None),
        P("row", "col", None, None),
        P("row", "col", None, None),
        P("row", "col", None, None, None),
        P("row", "col", None),
    )
    return jax.shard_map(
        on_device,
        mesh=mesh,
        in_specs=placed,
        out_specs=P("row", "col", None, None, None),
        check_vma=False,
    )
```

```python
import functools

import jax
import jax.numpy as jnp
from jax import lax
from jax.experimental import pallas as pl
from jax.experimental.pallas import tpu as pltpu
from jax.sharding import PartitionSpec as P

STOPS = 4


def passed_along(value, axis, steps):
    count = lax.axis_size(axis)
    pairs = [(source, (source + steps) % count) for source in range(count)]
    return lax.ppermute(value, axis, pairs)


def bucketize(blocks, index):
    picked = jnp.take(blocks, jnp.maximum(index, 0), axis=0)
    return jnp.where((index >= 0)[..., None, None], picked, jnp.zeros_like(picked))


GROUP = 32


def stop_kernel(stack_ref, map_ref, n_ref, left_ref, right_ref, acc_in_ref, acc_out_ref):
    live_count = n_ref[0]
    slots = map_ref.shape[0]
    left_count = left_ref.shape[0]
    right_count = right_ref.shape[0]
    result_count = acc_out_ref.shape[0]

    def per_group(g, carry):
        base = g * GROUP
        prods = []
        targets = []
        for k in range(GROUP):
            i = base + k
            slot = stack_ref[0, i]
            mapped = map_ref[jnp.clip(slot, 0, slots - 1)]
            ok = (i < live_count) & (slot >= 0) & (mapped >= 0)
            a = left_ref[jnp.clip(mapped, 0, left_count - 1)]
            b = right_ref[jnp.clip(stack_ref[1, i], 0, right_count - 1)]
            p = jnp.dot(a, b, preferred_element_type=jnp.float32)
            p = p.astype(jnp.bfloat16).astype(jnp.float32)
            prods.append(jnp.where(ok, p, 0.0))
            targets.append(jnp.clip(stack_ref[2, i], 0, result_count - 1))
        for k in range(GROUP):
            t = targets[k]
            acc_out_ref[t] = acc_out_ref[t] + prods[k]
        return carry

    acc_out_ref[...] = acc_in_ref[...]
    lax.fori_loop(0, (live_count + GROUP - 1) // GROUP, per_group, 0)


def run_stop(total, left, right, stack, left_map):
    slots = stack.shape[1]
    assert slots % GROUP == 0
    live_count = jnp.sum((stack[0] >= 0).astype(jnp.int32)).reshape(1)
    full = lambda shape: pl.BlockSpec(shape, lambda *_: (0,) * len(shape))
    grid_spec = pltpu.PrefetchScalarGridSpec(
        num_scalar_prefetch=3,
        grid=(1,),
        in_specs=[full(left.shape), full(right.shape), full(total.shape)],
        out_specs=full(total.shape),
    )
    return pl.pallas_call(
        stop_kernel,
        grid_spec=grid_spec,
        out_shape=jax.ShapeDtypeStruct(total.shape, jnp.float32),
        input_output_aliases={5: 0},
    )(stack.astype(jnp.int32), left_map, live_count, left, right, total)


def on_device(a_blocks, b_blocks, a_send, b_send, triples, c_send):
    rows_n = lax.axis_size("row")
    cols_n = lax.axis_size("col")
    count = rows_n * cols_n
    result_count = count // 2
    edge = a_blocks.shape[-1]
    held = a_blocks.shape[2]
    left_all = lax.all_gather(a_blocks[0, 0], "col", axis=0, tiled=True)
    send_all = lax.all_gather(a_send[0, 0], "col", axis=0, tiled=False)
    col_at = lax.axis_index("col")
    column_base = (jnp.arange(cols_n, dtype=jnp.int32) * held)[:, None]
    left_maps = []
    for stop_index in range(STOPS):
        owner = (col_at + stop_index) % cols_n
        picked = jnp.take(send_all, owner, axis=1)
        left_maps.append(jnp.where(picked >= 0, picked + column_base, -1).reshape(-1).astype(jnp.int32))
    right_out = bucketize(b_blocks[0, 0], b_send[0, 0])
    right_home = lax.all_to_all(right_out, "row", split_axis=0, concat_axis=0, tiled=True)
    right_home = right_home.reshape(-1, edge, edge)
    total = jnp.zeros((result_count, edge, edge), jnp.float32)
    rights = [right_home] + [passed_along(right_home, "row", -s) for s in range(1, STOPS)]
    for stop_index in range(STOPS):
        total = run_stop(total, left_all, rights[stop_index], triples[0, 0, stop_index], left_maps[stop_index])
    result = total.astype(jnp.bfloat16)
    outgoing = bucketize(result, c_send[0, 0])
    arrived = lax.all_to_all(outgoing, ("row", "col"), split_axis=0, concat_axis=0, tiled=True)
    return arrived[None, None]


def solution(mesh):
    placed = (
        P("row", "col", None, None, None),
        P("row", "col", None, None, None),
        P("row", "col", None, None),
        P("row", "col", None, None),
        P("row", "col", None, None, None),
        P("row", "col", None),
    )
    return jax.shard_map(
        on_device,
        mesh=mesh,
        in_specs=placed,
        out_specs=P("row", "col", None, None, None),
        check_vma=False,
    )
```

```python
import functools

import jax
import jax.numpy as jnp
from jax import lax
from jax.experimental import pallas as pl
from jax.experimental.pallas import tpu as pltpu
from jax.sharding import PartitionSpec as P

STOPS = 4


def passed_along(value, axis, steps):
    count = lax.axis_size(axis)
    pairs = [(source, (source + steps) % count) for source in range(count)]
    return lax.ppermute(value, axis, pairs)


def bucketize(blocks, index):
    picked = jnp.take(blocks, jnp.maximum(index, 0), axis=0)
    return jnp.where((index >= 0)[..., None, None], picked, jnp.zeros_like(picked))


GROUP = 32


def stop_kernel(ls_ref, rs_ref, ts_ref, n_ref, left_ref, right_ref, acc_in_ref, acc_out_ref):
    live_count = n_ref[0]

    def per_group(g, carry):
        base = g * GROUP
        prods = []
        for k in range(GROUP):
            i = base + k
            p = jnp.dot(left_ref[ls_ref[i]], right_ref[rs_ref[i]], preferred_element_type=jnp.float32)
            p = p.astype(jnp.bfloat16).astype(jnp.float32)
            prods.append(jnp.where(i < live_count, p, 0.0))
        for k in range(GROUP):
            t = ts_ref[base + k]
            acc_out_ref[t] = acc_out_ref[t] + prods[k]
        return carry

    acc_out_ref[...] = acc_in_ref[...]
    lax.fori_loop(0, (live_count + GROUP - 1) // GROUP, per_group, 0)


def run_stop(total, left, right, stack):
    result_count = total.shape[0]
    slots = stack.shape[1]
    assert slots % GROUP == 0
    ls = jnp.clip(stack[0], 0, left.shape[0] - 1).astype(jnp.int32)
    rs = jnp.clip(stack[1], 0, right.shape[0] - 1).astype(jnp.int32)
    ts = jnp.clip(stack[2], 0, result_count - 1).astype(jnp.int32)
    live_count = jnp.sum((stack[0] >= 0).astype(jnp.int32)).reshape(1)
    full = lambda shape: pl.BlockSpec(shape, lambda *_: (0,) * len(shape))
    grid_spec = pltpu.PrefetchScalarGridSpec(
        num_scalar_prefetch=4,
        grid=(1,),
        in_specs=[full(left.shape), full(right.shape), full(total.shape)],
        out_specs=full(total.shape),
    )
    return pl.pallas_call(
        stop_kernel,
        grid_spec=grid_spec,
        out_shape=jax.ShapeDtypeStruct(total.shape, jnp.float32),
        input_output_aliases={6: 0},
    )(ls, rs, ts, live_count, left, right, total)


def on_device(a_blocks, b_blocks, a_send, b_send, triples, c_send):
    rows_n = lax.axis_size("row")
    cols_n = lax.axis_size("col")
    count = rows_n * cols_n
    result_count = count // 2
    edge = a_blocks.shape[-1]
    left_out = bucketize(a_blocks[0, 0], a_send[0, 0])
    left_home = lax.all_to_all(left_out, "col", split_axis=0, concat_axis=0, tiled=True)
    left_home = left_home.reshape(-1, edge, edge)
    right_out = bucketize(b_blocks[0, 0], b_send[0, 0])
    right_home = lax.all_to_all(right_out, "row", split_axis=0, concat_axis=0, tiled=True)
    right_home = right_home.reshape(-1, edge, edge)
    total = jnp.zeros((result_count, edge, edge), jnp.float32)
    left_now = left_home
    right_now = right_home
    for stop_index in range(STOPS):
        if stop_index > 0:
            left_now = passed_along(left_now, "col", -1)
            right_now = passed_along(right_now, "row", -1)
        if stop_index > 0:
            left_now, right_now, total = lax.optimization_barrier((left_now, right_now, total))
        total = run_stop(total, left_now, right_now, triples[0, 0, stop_index])
    result = total.astype(jnp.bfloat16)
    outgoing = bucketize(result, c_send[0, 0])
    arrived = lax.all_to_all(outgoing, ("row", "col"), split_axis=0, concat_axis=0, tiled=True)
    return arrived[None, None]


def solution(mesh):
    placed = (
        P("row", "col", None, None, None),
        P("row", "col", None, None, None),
        P("row", "col", None, None),
        P("row", "col", None, None),
        P("row", "col", None, None, None),
        P("row", "col", None),
    )
    return jax.shard_map(
        on_device,
        mesh=mesh,
        in_specs=placed,
        out_specs=P("row", "col", None, None, None),
        check_vma=False,
    )
```

```python
import functools

import jax
import jax.numpy as jnp
from jax import lax
from jax.experimental import pallas as pl
from jax.experimental.pallas import tpu as pltpu
from jax.sharding import PartitionSpec as P

STOPS = 4


def passed_along(value, axis, steps):
    count = lax.axis_size(axis)
    pairs = [(source, (source + steps) % count) for source in range(count)]
    return lax.ppermute(value, axis, pairs)


def bucketize(blocks, index):
    picked = jnp.take(blocks, jnp.maximum(index, 0), axis=0)
    return jnp.where((index >= 0)[..., None, None], picked, jnp.zeros_like(picked))


GROUP = 32


def stop_kernel(stack_ref, map_ref, n_ref, left_ref, right_ref, acc_in_ref, acc_out_ref):
    live_count = n_ref[0]
    slots = map_ref.shape[0]
    left_count = left_ref.shape[0]
    right_count = right_ref.shape[0]
    result_count = acc_out_ref.shape[0]

    def per_group(g, carry):
        base = g * GROUP
        prods = []
        targets = []
        for k in range(GROUP):
            i = base + k
            slot = stack_ref[0, i]
            mapped = map_ref[jnp.clip(slot, 0, slots - 1)]
            ok = (i < live_count) & (slot >= 0) & (mapped >= 0)
            a = left_ref[jnp.clip(mapped, 0, left_count - 1)]
            b = right_ref[jnp.clip(stack_ref[1, i], 0, right_count - 1)]
            p = jnp.dot(a, b, preferred_element_type=jnp.float32)
            p = p.astype(jnp.bfloat16).astype(jnp.float32)
            prods.append(jnp.where(ok, p, 0.0))
            targets.append(jnp.clip(stack_ref[2, i], 0, result_count - 1))
        for k in range(GROUP):
            t = targets[k]
            acc_out_ref[t] = acc_out_ref[t] + prods[k]
        return carry

    acc_out_ref[...] = acc_in_ref[...]
    lax.fori_loop(0, (live_count + GROUP - 1) // GROUP, per_group, 0)


def run_stop(total, left, right, stack, left_map):
    slots = stack.shape[1]
    assert slots % GROUP == 0
    live_count = jnp.sum((stack[0] >= 0).astype(jnp.int32)).reshape(1)
    full = lambda shape: pl.BlockSpec(shape, lambda *_: (0,) * len(shape))
    grid_spec = pltpu.PrefetchScalarGridSpec(
        num_scalar_prefetch=3,
        grid=(1,),
        in_specs=[full(left.shape), full(right.shape), full(total.shape)],
        out_specs=full(total.shape),
    )
    return pl.pallas_call(
        stop_kernel,
        grid_spec=grid_spec,
        out_shape=jax.ShapeDtypeStruct(total.shape, jnp.float32),
        input_output_aliases={5: 0},
    )(stack.astype(jnp.int32), left_map, live_count, left, right, total)


def on_device(a_blocks, b_blocks, a_send, b_send, triples, c_send):
    rows_n = lax.axis_size("row")
    cols_n = lax.axis_size("col")
    count = rows_n * cols_n
    result_count = count // 2
    edge = a_blocks.shape[-1]
    left_out = bucketize(a_blocks[0, 0], a_send[0, 0])
    cap = left_out.shape[1]
    col_at = lax.axis_index("col")
    pieces = [jnp.take(left_out, col_at, axis=0)]
    for shift in range(1, cols_n):
        bucket = jnp.take(left_out, (col_at + shift) % cols_n, axis=0)
        pieces.append(passed_along(bucket, "col", shift))
    left_home = jnp.concatenate(pieces, axis=0)
    slot = jnp.arange(cols_n * cap, dtype=jnp.int32)
    left_maps = []
    for stop_index in range(STOPS):
        owner = (col_at + stop_index) % cols_n
        left_maps.append((((owner - slot // cap) % cols_n) * cap + slot % cap).astype(jnp.int32))
    right_out = bucketize(b_blocks[0, 0], b_send[0, 0])
    right_home = lax.all_to_all(right_out, "row", split_axis=0, concat_axis=0, tiled=True)
    right_home = right_home.reshape(-1, edge, edge)
    total = jnp.zeros((result_count, edge, edge), jnp.float32)
    left_now = left_home
    right_now = right_home
    for stop_index in range(STOPS):
        if stop_index > 0:
            left_now = passed_along(left_now, "col", -1)
            right_now = passed_along(right_now, "row", -1)
        if stop_index > 0:
            left_now, right_now, total = lax.optimization_barrier((left_now, right_now, total))
        total = run_stop(total, left_now, right_now, triples[0, 0, stop_index], left_maps[stop_index])
    result = total.astype(jnp.bfloat16)
    outgoing = bucketize(result, c_send[0, 0])
    arrived = lax.all_to_all(outgoing, ("row", "col"), split_axis=0, concat_axis=0, tiled=True)
    return arrived[None, None]


def solution(mesh):
    placed = (
        P("row", "col", None, None, None),
        P("row", "col", None, None, None),
        P("row", "col", None, None),
        P("row", "col", None, None),
        P("row", "col", None, None, None),
        P("row", "col", None),
    )
    return jax.shard_map(
        on_device,
        mesh=mesh,
        in_specs=placed,
        out_specs=P("row", "col", None, None, None),
        check_vma=False,
    )
```

```python
import functools

import jax
import jax.numpy as jnp
from jax import lax
from jax.experimental import pallas as pl
from jax.experimental.pallas import tpu as pltpu
from jax.sharding import PartitionSpec as P

STOPS = 4


def passed_along(value, axis, steps):
    count = lax.axis_size(axis)
    pairs = [(source, (source + steps) % count) for source in range(count)]
    return lax.ppermute(value, axis, pairs)


def bucketize(blocks, index):
    picked = jnp.take(blocks, jnp.maximum(index, 0), axis=0)
    return jnp.where((index >= 0)[..., None, None], picked, jnp.zeros_like(picked))


GROUP = 32


def stop_kernel(stop, first, last, stack_ref, map_ref, n_ref, left_ref, right_ref, *refs):
    if first:
        acc_out_ref, acc_ref = refs[0], refs[-1]
    else:
        acc_in_ref, acc_out_ref, acc_ref = refs[0], refs[1], refs[-1]
    live_count = n_ref[stop]
    slots = map_ref.shape[1]
    left_count = left_ref.shape[0]
    right_count = right_ref.shape[0]
    result_count = acc_out_ref.shape[0]

    def per_group(g, carry):
        base = g * GROUP
        prods = []
        targets = []
        for k in range(GROUP):
            i = base + k
            slot = stack_ref[stop, 0, i]
            mapped = map_ref[stop, jnp.clip(slot, 0, slots - 1)]
            ok = (i < live_count) & (slot >= 0) & (mapped >= 0)
            a = left_ref[jnp.clip(mapped, 0, left_count - 1)]
            b = right_ref[jnp.clip(stack_ref[stop, 1, i], 0, right_count - 1)]
            p = jnp.dot(a, b, preferred_element_type=jnp.float32)
            p = p.astype(jnp.bfloat16).astype(jnp.float32)
            prods.append(jnp.where(ok, p, 0.0))
            targets.append(jnp.clip(stack_ref[stop, 2, i], 0, result_count - 1))
        for k in range(GROUP):
            t = targets[k]
            acc_ref[t] = acc_ref[t] + prods[k]
        return carry

    if first:
        acc_ref[...] = jnp.zeros(acc_ref.shape, jnp.float32)
    else:
        acc_ref[...] = acc_in_ref[...]
    lax.fori_loop(0, (live_count + GROUP - 1) // GROUP, per_group, 0)
    acc_out_ref[...] = acc_ref[...].astype(acc_out_ref.dtype)


def run_stop(total, left, right, stacks, left_maps, live_counts, stop, last, result_shape):
    assert stacks.shape[-1] % GROUP == 0
    first = total is None
    full = lambda shape: pl.BlockSpec(shape, lambda *_: (0,) * len(shape))
    in_specs = [full(left.shape), full(right.shape)]
    operands = [stacks, left_maps, live_counts, left, right]
    aliases = {}
    if not first:
        in_specs.append(full(result_shape))
        operands.append(total)
        if not last:
            aliases = {5: 0}
    scratch = [pltpu.VMEM(result_shape, jnp.float32)]
    out_dtype = jnp.bfloat16 if last else jnp.float32
    grid_spec = pltpu.PrefetchScalarGridSpec(
        num_scalar_prefetch=3,
        grid=(1,),
        in_specs=in_specs,
        out_specs=full(result_shape),
        scratch_shapes=scratch,
    )
    return pl.pallas_call(
        functools.partial(stop_kernel, stop, first, last),
        grid_spec=grid_spec,
        out_shape=jax.ShapeDtypeStruct(result_shape, out_dtype),
        input_output_aliases=aliases,
    )(*operands)


def on_device(a_blocks, b_blocks, a_send, b_send, triples, c_send):
    rows_n = lax.axis_size("row")
    cols_n = lax.axis_size("col")
    count = rows_n * cols_n
    result_count = count // 2
    edge = a_blocks.shape[-1]
    left_out = bucketize(a_blocks[0, 0], a_send[0, 0])
    cap = left_out.shape[1]
    col_at = lax.axis_index("col")
    pieces = [jnp.take(left_out, col_at, axis=0)]
    for shift in range(1, cols_n):
        bucket = jnp.take(left_out, (col_at + shift) % cols_n, axis=0)
        pieces.append(passed_along(bucket, "col", shift))
    left_home = jnp.concatenate(pieces, axis=0)
    slot = jnp.arange(cols_n * cap, dtype=jnp.int32)[None, :]
    owner = (col_at + jnp.arange(STOPS, dtype=jnp.int32)[:, None]) % cols_n
    left_maps = (((owner - slot // cap) % cols_n) * cap + slot % cap).astype(jnp.int32)
    stacks = triples[0, 0].astype(jnp.int32)
    live_counts = jnp.sum((stacks[:, 0, :] >= 0).astype(jnp.int32), axis=1)
    right_out = bucketize(b_blocks[0, 0], b_send[0, 0])
    right_home = lax.all_to_all(right_out, "row", split_axis=0, concat_axis=0, tiled=True)
    right_home = right_home.reshape(-1, edge, edge)
    total = None
    result_shape = (result_count, edge, edge)
    left_now = left_home
    right_now = right_home
    for stop_index in range(STOPS):
        if stop_index > 0:
            left_now = passed_along(left_now, "col", -1)
            right_now = passed_along(right_now, "row", -1)
        if stop_index > 0:
            left_now, right_now, total = lax.optimization_barrier((left_now, right_now, total))
        total = run_stop(total, left_now, right_now, stacks, left_maps, live_counts, stop_index,
                         stop_index == STOPS - 1, result_shape)
    result = total
    outgoing = bucketize(result, c_send[0, 0])
    arrived = lax.all_to_all(outgoing, ("row", "col"), split_axis=0, concat_axis=0, tiled=True)
    return arrived[None, None]


def solution(mesh):
    placed = (
        P("row", "col", None, None, None),
        P("row", "col", None, None, None),
        P("row", "col", None, None),
        P("row", "col", None, None),
        P("row", "col", None, None, None),
        P("row", "col", None),
    )
    return jax.shard_map(
        on_device,
        mesh=mesh,
        in_specs=placed,
        out_specs=P("row", "col", None, None, None),
        check_vma=False,
    )
```

```python
import functools

import jax
import jax.numpy as jnp
from jax import lax
from jax.experimental import pallas as pl
from jax.experimental.pallas import tpu as pltpu
from jax.sharding import PartitionSpec as P

STOPS = 4


def passed_along(value, axis, steps):
    count = lax.axis_size(axis)
    pairs = [(source, (source + steps) % count) for source in range(count)]
    return lax.ppermute(value, axis, pairs)


def bucketize(blocks, index):
    picked = jnp.take(blocks, jnp.maximum(index, 0), axis=0)
    return jnp.where((index >= 0)[..., None, None], picked, jnp.zeros_like(picked))


GROUP = 64


def stop_kernel(stop, first, last, stack_ref, map_ref, n_ref, left_ref, right_ref, *refs):
    if first:
        acc_out_ref, acc_ref = refs[0], refs[-1]
    else:
        acc_in_ref, acc_out_ref, acc_ref = refs[0], refs[1], refs[-1]
    live_count = n_ref[stop]
    slots = map_ref.shape[1]
    left_count = left_ref.shape[0]
    right_count = right_ref.shape[0]
    result_count = acc_out_ref.shape[0]

    def per_group(g, carry):
        base = g * GROUP
        prods = []
        targets = []
        for k in range(GROUP):
            i = base + k
            slot = stack_ref[stop, 0, i]
            mapped = map_ref[stop, jnp.clip(slot, 0, slots - 1)]
            ok = (i < live_count) & (slot >= 0) & (mapped >= 0)
            a = left_ref[jnp.clip(mapped, 0, left_count - 1)]
            b = right_ref[jnp.clip(stack_ref[stop, 1, i], 0, right_count - 1)]
            p = jnp.dot(a, b, preferred_element_type=jnp.float32)
            p = p.astype(jnp.bfloat16).astype(jnp.float32)
            prods.append(jnp.where(ok, p, 0.0))
            targets.append(jnp.clip(stack_ref[stop, 2, i], 0, result_count - 1))
        for k in range(GROUP):
            t = targets[k]
            acc_ref[t] = acc_ref[t] + prods[k]
        return carry

    if first:
        acc_ref[...] = jnp.zeros(acc_ref.shape, jnp.float32)
    else:
        acc_ref[...] = acc_in_ref[...]
    lax.fori_loop(0, (live_count + GROUP - 1) // GROUP, per_group, 0)
    acc_out_ref[...] = acc_ref[...].astype(acc_out_ref.dtype)


def run_stop(total, left, right, stacks, left_maps, live_counts, stop, last, result_shape):
    assert stacks.shape[-1] % GROUP == 0
    first = total is None
    full = lambda shape: pl.BlockSpec(shape, lambda *_: (0,) * len(shape))
    in_specs = [full(left.shape), full(right.shape)]
    operands = [stacks, left_maps, live_counts, left, right]
    aliases = {}
    if not first:
        in_specs.append(full(result_shape))
        operands.append(total)
        if not last:
            aliases = {5: 0}
    scratch = [pltpu.VMEM(result_shape, jnp.float32)]
    out_dtype = jnp.bfloat16 if last else jnp.float32
    grid_spec = pltpu.PrefetchScalarGridSpec(
        num_scalar_prefetch=3,
        grid=(1,),
        in_specs=in_specs,
        out_specs=full(result_shape),
        scratch_shapes=scratch,
    )
    return pl.pallas_call(
        functools.partial(stop_kernel, stop, first, last),
        grid_spec=grid_spec,
        out_shape=jax.ShapeDtypeStruct(result_shape, out_dtype),
        input_output_aliases=aliases,
    )(*operands)


def on_device(a_blocks, b_blocks, a_send, b_send, triples, c_send):
    rows_n = lax.axis_size("row")
    cols_n = lax.axis_size("col")
    count = rows_n * cols_n
    result_count = count // 2
    edge = a_blocks.shape[-1]
    left_out = bucketize(a_blocks[0, 0], a_send[0, 0])
    cap = left_out.shape[1]
    col_at = lax.axis_index("col")
    pieces = [jnp.take(left_out, col_at, axis=0)]
    for shift in range(1, cols_n):
        bucket = jnp.take(left_out, (col_at + shift) % cols_n, axis=0)
        pieces.append(passed_along(bucket, "col", shift))
    left_home = jnp.concatenate(pieces, axis=0)
    slot = jnp.arange(cols_n * cap, dtype=jnp.int32)[None, :]
    owner = (col_at + jnp.arange(STOPS, dtype=jnp.int32)[:, None]) % cols_n
    left_maps = (((owner - slot // cap) % cols_n) * cap + slot % cap).astype(jnp.int32)
    stacks = triples[0, 0].astype(jnp.int32)
    live_counts = jnp.sum((stacks[:, 0, :] >= 0).astype(jnp.int32), axis=1)
    right_out = bucketize(b_blocks[0, 0], b_send[0, 0])
    right_home = lax.all_to_all(right_out, "row", split_axis=0, concat_axis=0, tiled=True)
    right_home = right_home.reshape(-1, edge, edge)
    total = None
    result_shape = (result_count, edge, edge)
    left_now = left_home
    right_now = right_home
    for stop_index in range(STOPS):
        if stop_index > 0:
            left_now = passed_along(left_now, "col", -1)
            right_now = passed_along(right_now, "row", -1)
        if stop_index > 0:
            left_now, right_now, total = lax.optimization_barrier((left_now, right_now, total))
        total = run_stop(total, left_now, right_now, stacks, left_maps, live_counts, stop_index,
                         stop_index == STOPS - 1, result_shape)
    result = total
    outgoing = bucketize(result, c_send[0, 0])
    arrived = lax.all_to_all(outgoing, ("row", "col"), split_axis=0, concat_axis=0, tiled=True)
    return arrived[None, None]


def solution(mesh):
    placed = (
        P("row", "col", None, None, None),
        P("row", "col", None, None, None),
        P("row", "col", None, None),
        P("row", "col", None, None),
        P("row", "col", None, None, None),
        P("row", "col", None),
    )
    return jax.shard_map(
        on_device,
        mesh=mesh,
        in_specs=placed,
        out_specs=P("row", "col", None, None, None),
        check_vma=False,
    )
```

```python
import functools

import jax
import jax.numpy as jnp
from jax import lax
from jax.experimental import pallas as pl
from jax.experimental.pallas import tpu as pltpu
from jax.sharding import PartitionSpec as P

STOPS = 4


def passed_along(value, axis, steps):
    count = lax.axis_size(axis)
    pairs = [(source, (source + steps) % count) for source in range(count)]
    return lax.ppermute(value, axis, pairs)


def bucketize(blocks, index):
    picked = jnp.take(blocks, jnp.maximum(index, 0), axis=0)
    return jnp.where((index >= 0)[..., None, None], picked, jnp.zeros_like(picked))


GROUP = 32


def stop_kernel(stop, first, last, stack_ref, map_ref, n_ref, send_ref, left_ref, right_ref, *refs):
    if first:
        acc_out_ref, acc_ref = refs[0], refs[-1]
    else:
        acc_in_ref, acc_out_ref, acc_ref = refs[0], refs[1], refs[-1]
    live_count = n_ref[stop]
    slots = map_ref.shape[1]
    left_count = left_ref.shape[0]
    right_count = right_ref.shape[0]
    result_count = acc_out_ref.shape[0]

    def per_group(g, carry):
        base = g * GROUP
        prods = []
        targets = []
        for k in range(GROUP):
            i = base + k
            slot = stack_ref[stop, 0, i]
            mapped = map_ref[stop, jnp.clip(slot, 0, slots - 1)]
            ok = (i < live_count) & (slot >= 0) & (mapped >= 0)
            a = left_ref[jnp.clip(mapped, 0, left_count - 1)]
            b = right_ref[jnp.clip(stack_ref[stop, 1, i], 0, right_count - 1)]
            p = jnp.dot(a, b, preferred_element_type=jnp.float32)
            p = p.astype(jnp.bfloat16).astype(jnp.float32)
            prods.append(jnp.where(ok, p, 0.0))
            targets.append(jnp.clip(stack_ref[stop, 2, i], 0, result_count - 1))
        for k in range(GROUP):
            t = targets[k]
            acc_ref[t] = acc_ref[t] + prods[k]
        return carry

    if first:
        acc_ref[...] = jnp.zeros(acc_ref.shape, jnp.float32)
    else:
        acc_ref[...] = acc_in_ref[...]
    lax.fori_loop(0, (live_count + GROUP - 1) // GROUP, per_group, 0)
    if last:
        def per_slot(e, carry):
            wanted = send_ref[e]
            block = acc_ref[jnp.clip(wanted, 0, result_count - 1)]
            acc_out_ref[e] = jnp.where(wanted >= 0, block, 0.0).astype(acc_out_ref.dtype)
            return carry

        lax.fori_loop(0, acc_out_ref.shape[0], per_slot, 0)
    else:
        acc_out_ref[...] = acc_ref[...]


def run_stop(total, left, right, stacks, left_maps, live_counts, c_send, stop, last, result_shape):
    assert stacks.shape[-1] % GROUP == 0
    first = total is None
    full = lambda shape: pl.BlockSpec(shape, lambda *_: (0,) * len(shape))
    in_specs = [full(left.shape), full(right.shape)]
    operands = [stacks, left_maps, live_counts, c_send, left, right]
    aliases = {}
    if not first:
        in_specs.append(full(result_shape))
        operands.append(total)
        if not last:
            aliases = {6: 0}
    scratch = [pltpu.VMEM(result_shape, jnp.float32)]
    out_dtype = jnp.bfloat16 if last else jnp.float32
    out_shape = (c_send.shape[0],) + result_shape[1:] if last else result_shape
    grid_spec = pltpu.PrefetchScalarGridSpec(
        num_scalar_prefetch=4,
        grid=(1,),
        in_specs=in_specs,
        out_specs=full(out_shape),
        scratch_shapes=scratch,
    )
    return pl.pallas_call(
        functools.partial(stop_kernel, stop, first, last),
        grid_spec=grid_spec,
        out_shape=jax.ShapeDtypeStruct(out_shape, out_dtype),
        input_output_aliases=aliases,
    )(*operands)


def on_device(a_blocks, b_blocks, a_send, b_send, triples, c_send):
    rows_n = lax.axis_size("row")
    cols_n = lax.axis_size("col")
    count = rows_n * cols_n
    result_count = count // 2
    edge = a_blocks.shape[-1]
    left_out = bucketize(a_blocks[0, 0], a_send[0, 0])
    cap = left_out.shape[1]
    col_at = lax.axis_index("col")
    pieces = [jnp.take(left_out, col_at, axis=0)]
    for shift in range(1, cols_n):
        bucket = jnp.take(left_out, (col_at + shift) % cols_n, axis=0)
        pieces.append(passed_along(bucket, "col", shift))
    left_home = jnp.concatenate(pieces, axis=0)
    slot = jnp.arange(cols_n * cap, dtype=jnp.int32)[None, :]
    owner = (col_at + jnp.arange(STOPS, dtype=jnp.int32)[:, None]) % cols_n
    left_maps = (((owner - slot // cap) % cols_n) * cap + slot % cap).astype(jnp.int32)
    stacks = triples[0, 0].astype(jnp.int32)
    live_counts = jnp.sum((stacks[:, 0, :] >= 0).astype(jnp.int32), axis=1)
    right_out = bucketize(b_blocks[0, 0], b_send[0, 0])
    right_home = lax.all_to_all(right_out, "row", split_axis=0, concat_axis=0, tiled=True)
    right_home = right_home.reshape(-1, edge, edge)
    total = None
    result_shape = (result_count, edge, edge)
    left_now = left_home
    right_now = right_home
    for stop_index in range(STOPS):
        if stop_index > 0:
            left_now = passed_along(left_now, "col", -1)
            right_now = passed_along(right_now, "row", -1)
        if stop_index > 0:
            left_now, right_now, total = lax.optimization_barrier((left_now, right_now, total))
        total = run_stop(total, left_now, right_now, stacks, left_maps, live_counts, c_send[0, 0], stop_index,
                         stop_index == STOPS - 1, result_shape)
    outgoing = total
    arrived = lax.all_to_all(outgoing, ("row", "col"), split_axis=0, concat_axis=0, tiled=True)
    return arrived[None, None]


def solution(mesh):
    placed = (
        P("row", "col", None, None, None),
        P("row", "col", None, None, None),
        P("row", "col", None, None),
        P("row", "col", None, None),
        P("row", "col", None, None, None),
        P("row", "col", None),
    )
    return jax.shard_map(
        on_device,
        mesh=mesh,
        in_specs=placed,
        out_specs=P("row", "col", None, None, None),
        check_vma=False,
    )
```

```python
import functools

import jax
import jax.numpy as jnp
from jax import lax
from jax.experimental import pallas as pl
from jax.experimental.pallas import tpu as pltpu
from jax.sharding import PartitionSpec as P

STOPS = 4


def passed_along(value, axis, steps):
    count = lax.axis_size(axis)
    pairs = [(source, (source + steps) % count) for source in range(count)]
    return lax.ppermute(value, axis, pairs)


def bucketize(blocks, index):
    picked = jnp.take(blocks, jnp.maximum(index, 0), axis=0)
    return jnp.where((index >= 0)[..., None, None], picked, jnp.zeros_like(picked))


GROUP = 32


def stop_kernel(stop, first, last, stack_ref, map_ref, n_ref, send_ref, left_ref, right_ref, *refs):
    if first:
        acc_out_ref, acc_ref = refs[0], refs[-1]
    else:
        acc_in_ref, acc_out_ref, acc_ref = refs[0], refs[1], refs[-1]
    live_count = n_ref[stop]
    slots = map_ref.shape[1]
    left_count = left_ref.shape[0]
    right_count = right_ref.shape[0]
    result_count = acc_out_ref.shape[0]

    def per_group(g, carry):
        base = g * GROUP
        prods = []
        targets = []
        for k in range(GROUP):
            i = base + k
            slot = stack_ref[stop, 0, i]
            mapped = map_ref[stop, jnp.clip(slot, 0, slots - 1)]
            ok = (i < live_count) & (slot >= 0) & (mapped >= 0)
            a = left_ref[jnp.clip(mapped, 0, left_count - 1)]
            b = right_ref[jnp.clip(stack_ref[stop, 1, i], 0, right_count - 1)]
            p = jnp.dot(a, b, preferred_element_type=jnp.float32)
            p = p.astype(jnp.bfloat16).astype(jnp.float32)
            prods.append(jnp.where(ok, p, 0.0))
            targets.append(jnp.clip(stack_ref[stop, 2, i], 0, result_count - 1))
        for k in range(GROUP):
            t = targets[k]
            acc_ref[t] = acc_ref[t] + prods[k]
        return carry

    if first:
        acc_ref[...] = jnp.zeros(acc_ref.shape, jnp.float32)
    else:
        acc_ref[...] = acc_in_ref[...]
    lax.fori_loop(0, (live_count + GROUP - 1) // GROUP, per_group, 0)
    if last:
        for e in range(acc_out_ref.shape[0]):
            wanted = send_ref[e]
            block = acc_ref[jnp.clip(wanted, 0, result_count - 1)].astype(acc_out_ref.dtype)
            acc_out_ref[e] = jnp.where(wanted >= 0, block, jnp.zeros_like(block))
    else:
        acc_out_ref[...] = acc_ref[...]


def run_stop(total, left, right, stacks, left_maps, live_counts, c_send, stop, last, result_shape):
    assert stacks.shape[-1] % GROUP == 0
    first = total is None
    full = lambda shape: pl.BlockSpec(shape, lambda *_: (0,) * len(shape))
    in_specs = [full(left.shape), full(right.shape)]
    operands = [stacks, left_maps, live_counts, c_send, left, right]
    aliases = {}
    if not first:
        in_specs.append(full(result_shape))
        operands.append(total)
        if not last:
            aliases = {6: 0}
    scratch = [pltpu.VMEM(result_shape, jnp.float32)]
    out_dtype = jnp.bfloat16 if last else jnp.float32
    out_shape = (c_send.shape[0],) + result_shape[1:] if last else result_shape
    grid_spec = pltpu.PrefetchScalarGridSpec(
        num_scalar_prefetch=4,
        grid=(1,),
        in_specs=in_specs,
        out_specs=full(out_shape),
        scratch_shapes=scratch,
    )
    return pl.pallas_call(
        functools.partial(stop_kernel, stop, first, last),
        grid_spec=grid_spec,
        out_shape=jax.ShapeDtypeStruct(out_shape, out_dtype),
        input_output_aliases=aliases,
    )(*operands)


def on_device(a_blocks, b_blocks, a_send, b_send, triples, c_send):
    rows_n = lax.axis_size("row")
    cols_n = lax.axis_size("col")
    count = rows_n * cols_n
    result_count = count // 2
    edge = a_blocks.shape[-1]
    left_out = bucketize(a_blocks[0, 0], a_send[0, 0])
    cap = left_out.shape[1]
    col_at = lax.axis_index("col")
    pieces = [jnp.take(left_out, col_at, axis=0)]
    for shift in range(1, cols_n):
        bucket = jnp.take(left_out, (col_at + shift) % cols_n, axis=0)
        pieces.append(passed_along(bucket, "col", shift))
    left_home = jnp.concatenate(pieces, axis=0)
    slot = jnp.arange(cols_n * cap, dtype=jnp.int32)[None, :]
    owner = (col_at + jnp.arange(STOPS, dtype=jnp.int32)[:, None]) % cols_n
    left_maps = (((owner - slot // cap) % cols_n) * cap + slot % cap).astype(jnp.int32)
    stacks = triples[0, 0].astype(jnp.int32)
    live_counts = jnp.sum((stacks[:, 0, :] >= 0).astype(jnp.int32), axis=1)
    right_out = bucketize(b_blocks[0, 0], b_send[0, 0])
    right_home = lax.all_to_all(right_out, "row", split_axis=0, concat_axis=0, tiled=True)
    right_home = right_home.reshape(-1, edge, edge)
    total = None
    result_shape = (result_count, edge, edge)
    left_now = left_home
    right_now = right_home
    for stop_index in range(STOPS):
        if stop_index > 0:
            left_now = passed_along(left_now, "col", -1)
            right_now = passed_along(right_now, "row", -1)
        if stop_index > 0:
            left_now, right_now, total = lax.optimization_barrier((left_now, right_now, total))
        total = run_stop(total, left_now, right_now, stacks, left_maps, live_counts, c_send[0, 0], stop_index,
                         stop_index == STOPS - 1, result_shape)
    outgoing = total
    return lax.all_to_all(outgoing[None, None], ("row", "col"), split_axis=2, concat_axis=2, tiled=True)


def solution(mesh):
    placed = (
        P("row", "col", None, None, None),
        P("row", "col", None, None, None),
        P("row", "col", None, None),
        P("row", "col", None, None),
        P("row", "col", None, None, None),
        P("row", "col", None),
    )
    return jax.shard_map(
        on_device,
        mesh=mesh,
        in_specs=placed,
        out_specs=P("row", "col", None, None, None),
        check_vma=False,
    )
```

```python
import functools

import jax
import jax.numpy as jnp
from jax import lax
from jax.experimental import pallas as pl
from jax.experimental.pallas import tpu as pltpu
from jax.sharding import PartitionSpec as P

STOPS = 4


def passed_along(value, axis, steps):
    count = lax.axis_size(axis)
    pairs = [(source, (source + steps) % count) for source in range(count)]
    return lax.ppermute(value, axis, pairs)


def bucketize(blocks, index):
    picked = jnp.take(blocks, jnp.maximum(index, 0), axis=0)
    return jnp.where((index >= 0)[..., None, None], picked, jnp.zeros_like(picked))


GROUP = 32


def stop_kernel(stop, first, last, stack_ref, map_ref, n_ref, send_ref, left_ref, right_ref, *refs):
    if first:
        acc_out_ref, acc_ref = refs[0], refs[-1]
    else:
        acc_in_ref, acc_out_ref, acc_ref = refs[0], refs[1], refs[-1]
    live_count = n_ref[stop]
    slots = map_ref.shape[1]
    left_count = left_ref.shape[0]
    right_count = right_ref.shape[0]
    result_count = acc_out_ref.shape[0]

    def per_group(g, carry):
        base = g * GROUP
        prods = []
        targets = []
        for k in range(GROUP):
            i = base + k
            slot = stack_ref[stop, 0, i]
            mapped = map_ref[stop, jnp.clip(slot, 0, slots - 1)]
            ok = (i < live_count) & (slot >= 0) & (mapped >= 0)
            a = left_ref[jnp.clip(mapped, 0, left_count - 1)]
            b = right_ref[jnp.clip(stack_ref[stop, 1, i], 0, right_count - 1)]
            p = jnp.dot(a, b, preferred_element_type=jnp.float32)
            p = p.astype(jnp.bfloat16).astype(jnp.float32)
            prods.append(jnp.where(ok, p, 0.0))
            targets.append(jnp.clip(stack_ref[stop, 2, i], 0, result_count - 1))
        for k in range(GROUP):
            t = targets[k]
            acc_ref[t] = acc_ref[t] + prods[k]
        return carry

    if first:
        acc_ref[...] = jnp.zeros(acc_ref.shape, jnp.float32)
    else:
        acc_ref[...] = acc_in_ref[...]
    lax.fori_loop(0, (live_count + GROUP - 1) // GROUP, per_group, 0)
    if last:
        for e in range(acc_out_ref.shape[0]):
            wanted = send_ref[e]
            block = acc_ref[jnp.clip(wanted, 0, result_count - 1)].astype(acc_out_ref.dtype)
            acc_out_ref[e] = jnp.where(wanted >= 0, block, jnp.zeros_like(block))
    else:
        acc_out_ref[...] = acc_ref[...]


def run_stop(total, left, right, stacks, left_maps, live_counts, c_send, stop, last, result_shape):
    assert stacks.shape[-1] % GROUP == 0
    first = total is None
    full = lambda shape: pl.BlockSpec(shape, lambda *_: (0,) * len(shape))
    in_specs = [full(left.shape), full(right.shape)]
    operands = [stacks, left_maps, live_counts, c_send, left, right]
    aliases = {}
    if not first:
        in_specs.append(full(result_shape))
        operands.append(total)
        if not last:
            aliases = {6: 0}
    scratch = [pltpu.VMEM(result_shape, jnp.float32)]
    out_dtype = jnp.bfloat16 if last else jnp.float32
    out_shape = (c_send.shape[0],) + result_shape[1:] if last else result_shape
    grid_spec = pltpu.PrefetchScalarGridSpec(
        num_scalar_prefetch=4,
        grid=(1,),
        in_specs=in_specs,
        out_specs=full(out_shape),
        scratch_shapes=scratch,
    )
    return pl.pallas_call(
        functools.partial(stop_kernel, stop, first, last),
        grid_spec=grid_spec,
        out_shape=jax.ShapeDtypeStruct(out_shape, out_dtype),
        input_output_aliases=aliases,
    )(*operands)


def on_device(a_blocks, b_blocks, a_send, b_send, triples, c_send):
    rows_n = lax.axis_size("row")
    cols_n = lax.axis_size("col")
    count = rows_n * cols_n
    result_count = count // 2
    edge = a_blocks.shape[-1]
    left_out = bucketize(a_blocks[0, 0], a_send[0, 0])
    cap = left_out.shape[1]
    col_at = lax.axis_index("col")
    pieces = [jnp.take(left_out, col_at, axis=0)]
    for shift in range(1, cols_n):
        bucket = jnp.take(left_out, (col_at + shift) % cols_n, axis=0)
        pieces.append(passed_along(bucket, "col", shift))
    left_home = jnp.concatenate(pieces, axis=0)
    slot = jnp.arange(cols_n * cap, dtype=jnp.int32)[None, :]
    owner = (col_at + jnp.arange(STOPS, dtype=jnp.int32)[:, None]) % cols_n
    left_maps = (((owner - slot // cap) % cols_n) * cap + slot % cap).astype(jnp.int32)
    stacks = triples[0, 0].astype(jnp.int32)
    live_counts = jnp.sum((stacks[:, 0, :] >= 0).astype(jnp.int32), axis=1)
    right_out = bucketize(b_blocks[0, 0], b_send[0, 0])
    right_home = lax.all_to_all(right_out, "row", split_axis=0, concat_axis=0, tiled=True)
    right_home = right_home.reshape(-1, edge, edge)
    total = None
    result_shape = (result_count, edge, edge)
    left_now = left_home
    rights = [right_home] + [passed_along(right_home, "row", -s) for s in range(1, STOPS)]
    for stop_index in range(STOPS):
        right_now = rights[stop_index]
        if stop_index > 0:
            left_now = passed_along(left_now, "col", -1)
            left_now, total = lax.optimization_barrier((left_now, total))
        total = run_stop(total, left_now, right_now, stacks, left_maps, live_counts, c_send[0, 0], stop_index,
                         stop_index == STOPS - 1, result_shape)
    outgoing = total
    return lax.all_to_all(outgoing[None, None], ("row", "col"), split_axis=2, concat_axis=2, tiled=True)


def solution(mesh):
    placed = (
        P("row", "col", None, None, None),
        P("row", "col", None, None, None),
        P("row", "col", None, None),
        P("row", "col", None, None),
        P("row", "col", None, None, None),
        P("row", "col", None),
    )
    return jax.shard_map(
        on_device,
        mesh=mesh,
        in_specs=placed,
        out_specs=P("row", "col", None, None, None),
        check_vma=False,
    )
```

```python
import functools

import jax
import jax.numpy as jnp
from jax import lax
from jax.experimental import pallas as pl
from jax.experimental.pallas import tpu as pltpu
from jax.sharding import PartitionSpec as P

STOPS = 4


def passed_along(value, axis, steps):
    count = lax.axis_size(axis)
    pairs = [(source, (source + steps) % count) for source in range(count)]
    return lax.ppermute(value, axis, pairs)


def bucketize(blocks, index):
    picked = jnp.take(blocks, jnp.maximum(index, 0), axis=0)
    return jnp.where((index >= 0)[..., None, None], picked, jnp.zeros_like(picked))


GROUP = 32


def stop_kernel(stop, first, last, stack_ref, map_ref, n_ref, send_ref, left_ref, right_ref, *refs):
    if first:
        acc_out_ref, acc_ref = refs[0], refs[-1]
    else:
        acc_in_ref, acc_out_ref, acc_ref = refs[0], refs[1], refs[-1]
    live_count = n_ref[stop]
    slots = map_ref.shape[1]
    left_count = left_ref.shape[0]
    right_count = right_ref.shape[0]
    result_count = acc_out_ref.shape[0]

    def per_group(g, carry):
        base = g * GROUP
        prods = []
        targets = []
        for k in range(GROUP):
            i = base + k
            a = left_ref[stack_ref[stop, 0, i]]
            b = right_ref[stack_ref[stop, 1, i]]
            p = jnp.dot(a, b, preferred_element_type=jnp.float32)
            p = p.astype(jnp.bfloat16).astype(jnp.float32)
            prods.append(jnp.where((i < live_count) & (stack_ref[stop, 3, i] > 0), p, 0.0))
            targets.append(stack_ref[stop, 2, i])
        for k in range(GROUP):
            t = targets[k]
            acc_ref[t] = acc_ref[t] + prods[k]
        return carry

    if first:
        acc_ref[...] = jnp.zeros(acc_ref.shape, jnp.float32)
    else:
        acc_ref[...] = acc_in_ref[...]
    lax.fori_loop(0, (live_count + GROUP - 1) // GROUP, per_group, 0)
    if last:
        for e in range(acc_out_ref.shape[0]):
            wanted = send_ref[e]
            block = acc_ref[jnp.clip(wanted, 0, result_count - 1)].astype(acc_out_ref.dtype)
            acc_out_ref[e] = jnp.where(wanted >= 0, block, jnp.zeros_like(block))
    else:
        acc_out_ref[...] = acc_ref[...]


def run_stop(total, left, right, stacks, left_maps, live_counts, c_send, stop, last, result_shape):
    assert stacks.shape[-1] % GROUP == 0
    first = total is None
    full = lambda shape: pl.BlockSpec(shape, lambda *_: (0,) * len(shape))
    in_specs = [full(left.shape), full(right.shape)]
    operands = [stacks, left_maps, live_counts, c_send, left, right]
    aliases = {}
    if not first:
        in_specs.append(full(result_shape))
        operands.append(total)
        if not last:
            aliases = {6: 0}
    scratch = [pltpu.VMEM(result_shape, jnp.float32)]
    out_dtype = jnp.bfloat16 if last else jnp.float32
    out_shape = (c_send.shape[0],) + result_shape[1:] if last else result_shape
    grid_spec = pltpu.PrefetchScalarGridSpec(
        num_scalar_prefetch=4,
        grid=(1,),
        in_specs=in_specs,
        out_specs=full(out_shape),
        scratch_shapes=scratch,
    )
    return pl.pallas_call(
        functools.partial(stop_kernel, stop, first, last),
        grid_spec=grid_spec,
        out_shape=jax.ShapeDtypeStruct(out_shape, out_dtype),
        input_output_aliases=aliases,
    )(*operands)


def on_device(a_blocks, b_blocks, a_send, b_send, triples, c_send):
    rows_n = lax.axis_size("row")
    cols_n = lax.axis_size("col")
    count = rows_n * cols_n
    result_count = count // 2
    edge = a_blocks.shape[-1]
    left_out = bucketize(a_blocks[0, 0], a_send[0, 0])
    cap = left_out.shape[1]
    col_at = lax.axis_index("col")
    pieces = [jnp.take(left_out, col_at, axis=0)]
    for shift in range(1, cols_n):
        bucket = jnp.take(left_out, (col_at + shift) % cols_n, axis=0)
        pieces.append(passed_along(bucket, "col", shift))
    left_home = jnp.concatenate(pieces, axis=0)
    stacks = triples[0, 0].astype(jnp.int32)
    owner = (col_at + jnp.arange(STOPS, dtype=jnp.int32)[:, None]) % cols_n
    slot = jnp.clip(stacks[:, 0, :], 0, cols_n * cap - 1)
    left_index = ((owner - slot // cap) % cols_n) * cap + slot % cap
    right_index = jnp.clip(stacks[:, 1, :], 0, rows_n * b_send.shape[-1] - 1)
    target_index = jnp.clip(stacks[:, 2, :], 0, result_count - 1)
    live = (stacks[:, 0, :] >= 0).astype(jnp.int32)
    stacks = jnp.stack([left_index, right_index, target_index, live], axis=1).astype(jnp.int32)
    left_maps = jnp.zeros((STOPS, 1), jnp.int32)
    live_counts = jnp.sum(live, axis=1)
    right_out = bucketize(b_blocks[0, 0], b_send[0, 0])
    right_home = lax.all_to_all(right_out, "row", split_axis=0, concat_axis=0, tiled=True)
    right_home = right_home.reshape(-1, edge, edge)
    total = None
    result_shape = (result_count, edge, edge)
    left_now = left_home
    rights = [right_home] + [passed_along(right_home, "row", -s) for s in range(1, STOPS)]
    for stop_index in range(STOPS):
        right_now = rights[stop_index]
        if stop_index > 0:
            left_now = passed_along(left_now, "col", -1)
            left_now, total = lax.optimization_barrier((left_now, total))
        total = run_stop(total, left_now, right_now, stacks, left_maps, live_counts, c_send[0, 0], stop_index,
                         stop_index == STOPS - 1, result_shape)
    outgoing = total
    return lax.all_to_all(outgoing[None, None], ("row", "col"), split_axis=2, concat_axis=2, tiled=True)


def solution(mesh):
    placed = (
        P("row", "col", None, None, None),
        P("row", "col", None, None, None),
        P("row", "col", None, None),
        P("row", "col", None, None),
        P("row", "col", None, None, None),
        P("row", "col", None),
    )
    return jax.shard_map(
        on_device,
        mesh=mesh,
        in_specs=placed,
        out_specs=P("row", "col", None, None, None),
        check_vma=False,
    )
```

```python
import functools

import jax
import jax.numpy as jnp
from jax import lax
from jax.experimental import pallas as pl
from jax.experimental.pallas import tpu as pltpu
from jax.sharding import PartitionSpec as P

STOPS = 4


def passed_along(value, axis, steps):
    count = lax.axis_size(axis)
    pairs = [(source, (source + steps) % count) for source in range(count)]
    return lax.ppermute(value, axis, pairs)


def bucketize(blocks, index):
    picked = jnp.take(blocks, jnp.maximum(index, 0), axis=0)
    return jnp.where((index >= 0)[..., None, None], picked, jnp.zeros_like(picked))


GROUP = 32


def stop_kernel(stop, first, last, stack_ref, map_ref, n_ref, send_ref, left_ref, right_ref, *refs):
    if first:
        acc_out_ref, acc_ref = refs[0], refs[-1]
    else:
        acc_in_ref, acc_out_ref, acc_ref = refs[0], refs[1], refs[-1]
    live_count = n_ref[stop]
    slots = map_ref.shape[1]
    left_count = left_ref.shape[0]
    right_count = right_ref.shape[0]
    result_count = acc_out_ref.shape[0]

    def per_group(g, carry):
        base = g * GROUP
        prods = []
        targets = []
        for k in range(GROUP):
            i = base + k
            a = left_ref[stack_ref[stop, 0, i]]
            b = right_ref[stack_ref[stop, 1, i]]
            p = jnp.dot(a, b, preferred_element_type=jnp.float32)
            p = p.astype(jnp.bfloat16).astype(jnp.float32)
            prods.append(jnp.where((i < live_count) & (stack_ref[stop, 3, i] > 0), p, 0.0))
            targets.append(stack_ref[stop, 2, i])
        for k in range(GROUP):
            t = targets[k]
            acc_ref[t] = acc_ref[t] + prods[k]
        return carry

    if first:
        acc_ref[...] = jnp.zeros(acc_ref.shape, jnp.float32)
    else:
        acc_ref[...] = acc_in_ref[...]
    lax.fori_loop(0, (live_count + GROUP - 1) // GROUP, per_group, 0)
    if last:
        for e in range(acc_out_ref.shape[0]):
            wanted = send_ref[e]
            block = acc_ref[jnp.clip(wanted, 0, result_count - 1)].astype(acc_out_ref.dtype)
            acc_out_ref[e] = jnp.where(wanted >= 0, block, jnp.zeros_like(block))
    else:
        acc_out_ref[...] = acc_ref[...]


def run_stop(total, left, right, stacks, left_maps, live_counts, c_send, stop, last, result_shape):
    assert stacks.shape[-1] % GROUP == 0
    first = total is None
    full = lambda shape: pl.BlockSpec(shape, lambda *_: (0,) * len(shape))
    in_specs = [full(left.shape), full(right.shape)]
    operands = [stacks, left_maps, live_counts, c_send, left, right]
    aliases = {}
    if not first:
        in_specs.append(full(result_shape))
        operands.append(total)
        if not last:
            aliases = {6: 0}
    scratch = [pltpu.VMEM(result_shape, jnp.float32)]
    out_dtype = jnp.bfloat16 if last else jnp.float32
    out_shape = (c_send.shape[0],) + result_shape[1:] if last else result_shape
    grid_spec = pltpu.PrefetchScalarGridSpec(
        num_scalar_prefetch=4,
        grid=(1,),
        in_specs=in_specs,
        out_specs=full(out_shape),
        scratch_shapes=scratch,
    )
    return pl.pallas_call(
        functools.partial(stop_kernel, stop, first, last),
        grid_spec=grid_spec,
        out_shape=jax.ShapeDtypeStruct(out_shape, out_dtype),
        input_output_aliases=aliases,
    )(*operands)


def on_device(a_blocks, b_blocks, a_send, b_send, triples, c_send):
    rows_n = lax.axis_size("row")
    cols_n = lax.axis_size("col")
    count = rows_n * cols_n
    result_count = count // 2
    edge = a_blocks.shape[-1]
    left_out = bucketize(a_blocks[0, 0], a_send[0, 0])
    cap = left_out.shape[1]
    col_at = lax.axis_index("col")
    pieces = [jnp.take(left_out, col_at, axis=0)]
    for shift in range(1, cols_n):
        bucket = jnp.take(left_out, (col_at + shift) % cols_n, axis=0)
        pieces.append(passed_along(bucket, "col", shift))
    left_home = jnp.concatenate(pieces, axis=0)
    stacks = triples[0, 0].astype(jnp.int32)
    owner = (col_at + jnp.arange(STOPS, dtype=jnp.int32)[:, None]) % cols_n
    slot = jnp.clip(stacks[:, 0, :], 0, cols_n * cap - 1)
    left_index = ((owner - slot // cap) % cols_n) * cap + slot % cap
    right_index = jnp.clip(stacks[:, 1, :], 0, rows_n * b_send.shape[-1] - 1)
    target_index = jnp.clip(stacks[:, 2, :], 0, result_count - 1)
    live = (stacks[:, 0, :] >= 0).astype(jnp.int32)
    stacks = jnp.stack([left_index, right_index, target_index, live], axis=1).astype(jnp.int32)
    left_maps = jnp.zeros((STOPS, 1), jnp.int32)
    live_counts = jnp.sum(live, axis=1)
    right_out = bucketize(b_blocks[0, 0], b_send[0, 0])
    right_home = lax.all_to_all(right_out, "row", split_axis=0, concat_axis=0, tiled=True)
    right_home = right_home.reshape(-1, edge, edge)
    total = None
    result_shape = (result_count, edge, edge)
    left_home, right_home = lax.optimization_barrier((left_home, right_home))
    left_now = left_home
    rights = [right_home] + [passed_along(right_home, "row", -s) for s in range(1, STOPS)]
    for stop_index in range(STOPS):
        right_now = rights[stop_index]
        if stop_index > 0:
            left_now = passed_along(left_now, "col", -1)
            left_now, total = lax.optimization_barrier((left_now, total))
        total = run_stop(total, left_now, right_now, stacks, left_maps, live_counts, c_send[0, 0], stop_index,
                         stop_index == STOPS - 1, result_shape)
    outgoing = total
    return lax.all_to_all(outgoing[None, None], ("row", "col"), split_axis=2, concat_axis=2, tiled=True)


def solution(mesh):
    placed = (
        P("row", "col", None, None, None),
        P("row", "col", None, None, None),
        P("row", "col", None, None),
        P("row", "col", None, None),
        P("row", "col", None, None, None),
        P("row", "col", None),
    )
    return jax.shard_map(
        on_device,
        mesh=mesh,
        in_specs=placed,
        out_specs=P("row", "col", None, None, None),
        check_vma=False,
    )
```

```python
import functools

import jax
import jax.numpy as jnp
from jax import lax
from jax.experimental import pallas as pl
from jax.experimental.pallas import tpu as pltpu
from jax.sharding import PartitionSpec as P

STOPS = 4


def passed_along(value, axis, steps):
    count = lax.axis_size(axis)
    pairs = [(source, (source + steps) % count) for source in range(count)]
    return lax.ppermute(value, axis, pairs)


def bucketize(blocks, index):
    picked = jnp.take(blocks, jnp.maximum(index, 0), axis=0)
    return jnp.where((index >= 0)[..., None, None], picked, jnp.zeros_like(picked))


GROUP = 32


def stop_kernel(stop, first, last, stack_ref, map_ref, n_ref, send_ref, left_ref, right_ref, *refs):
    if first:
        acc_out_ref = refs[0]
        acc_ref = refs[-1] if last else acc_out_ref
    else:
        acc_in_ref, acc_out_ref = refs[0], refs[1]
        acc_ref = refs[-1] if last else acc_out_ref
    live_count = n_ref[stop]
    slots = map_ref.shape[1]
    left_count = left_ref.shape[0]
    right_count = right_ref.shape[0]
    result_count = acc_out_ref.shape[0]

    def per_group(g, carry):
        base = g * GROUP
        prods = []
        targets = []
        for k in range(GROUP):
            i = base + k
            slot = stack_ref[stop, 0, i]
            mapped = map_ref[stop, jnp.clip(slot, 0, slots - 1)]
            ok = (i < live_count) & (slot >= 0) & (mapped >= 0)
            a = left_ref[jnp.clip(mapped, 0, left_count - 1)]
            b = right_ref[jnp.clip(stack_ref[stop, 1, i], 0, right_count - 1)]
            p = jnp.dot(a, b, preferred_element_type=jnp.float32)
            p = p.astype(jnp.bfloat16).astype(jnp.float32)
            prods.append(jnp.where(ok, p, 0.0))
            targets.append(jnp.clip(stack_ref[stop, 2, i], 0, result_count - 1))
        for k in range(GROUP):
            t = targets[k]
            acc_ref[t] = acc_ref[t] + prods[k]
        return carry

    if first:
        acc_ref[...] = jnp.zeros(acc_ref.shape, jnp.float32)
    else:
        acc_ref[...] = acc_in_ref[...]
    lax.fori_loop(0, (live_count + GROUP - 1) // GROUP, per_group, 0)
    if last:
        for e in range(acc_out_ref.shape[0]):
            wanted = send_ref[e]
            block = acc_ref[jnp.clip(wanted, 0, result_count - 1)].astype(acc_out_ref.dtype)
            acc_out_ref[e] = jnp.where(wanted >= 0, block, jnp.zeros_like(block))


def run_stop(total, left, right, stacks, left_maps, live_counts, c_send, stop, last, result_shape):
    assert stacks.shape[-1] % GROUP == 0
    first = total is None
    full = lambda shape: pl.BlockSpec(shape, lambda *_: (0,) * len(shape))
    in_specs = [full(left.shape), full(right.shape)]
    operands = [stacks, left_maps, live_counts, c_send, left, right]
    aliases = {}
    if not first:
        in_specs.append(full(result_shape))
        operands.append(total)
        if not last:
            aliases = {6: 0}
    scratch = [pltpu.VMEM(result_shape, jnp.float32)] if last else []
    out_dtype = jnp.bfloat16 if last else jnp.float32
    out_shape = (c_send.shape[0],) + result_shape[1:] if last else result_shape
    grid_spec = pltpu.PrefetchScalarGridSpec(
        num_scalar_prefetch=4,
        grid=(1,),
        in_specs=in_specs,
        out_specs=full(out_shape),
        scratch_shapes=scratch,
    )
    return pl.pallas_call(
        functools.partial(stop_kernel, stop, first, last),
        grid_spec=grid_spec,
        out_shape=jax.ShapeDtypeStruct(out_shape, out_dtype),
        input_output_aliases=aliases,
    )(*operands)


def on_device(a_blocks, b_blocks, a_send, b_send, triples, c_send):
    rows_n = lax.axis_size("row")
    cols_n = lax.axis_size("col")
    count = rows_n * cols_n
    result_count = count // 2
    edge = a_blocks.shape[-1]
    left_out = bucketize(a_blocks[0, 0], a_send[0, 0])
    cap = left_out.shape[1]
    col_at = lax.axis_index("col")
    pieces = [jnp.take(left_out, col_at, axis=0)]
    for shift in range(1, cols_n):
        bucket = jnp.take(left_out, (col_at + shift) % cols_n, axis=0)
        pieces.append(passed_along(bucket, "col", shift))
    left_home = jnp.concatenate(pieces, axis=0)
    slot = jnp.arange(cols_n * cap, dtype=jnp.int32)[None, :]
    owner = (col_at + jnp.arange(STOPS, dtype=jnp.int32)[:, None]) % cols_n
    left_maps = (((owner - slot // cap) % cols_n) * cap + slot % cap).astype(jnp.int32)
    stacks = triples[0, 0].astype(jnp.int32)
    live_counts = jnp.sum((stacks[:, 0, :] >= 0).astype(jnp.int32), axis=1)
    right_out = bucketize(b_blocks[0, 0], b_send[0, 0])
    right_home = lax.all_to_all(right_out, "row", split_axis=0, concat_axis=0, tiled=True)
    right_home = right_home.reshape(-1, edge, edge)
    total = None
    result_shape = (result_count, edge, edge)
    left_now = left_home
    rights = [right_home] + [passed_along(right_home, "row", -s) for s in range(1, STOPS)]
    for stop_index in range(STOPS):
        right_now = rights[stop_index]
        if stop_index > 0:
            left_now = passed_along(left_now, "col", -1)
            left_now, total = lax.optimization_barrier((left_now, total))
        total = run_stop(total, left_now, right_now, stacks, left_maps, live_counts, c_send[0, 0], stop_index,
                         stop_index == STOPS - 1, result_shape)
    outgoing = total
    return lax.all_to_all(outgoing[None, None], ("row", "col"), split_axis=2, concat_axis=2, tiled=True)


def solution(mesh):
    placed = (
        P("row", "col", None, None, None),
        P("row", "col", None, None, None),
        P("row", "col", None, None),
        P("row", "col", None, None),
        P("row", "col", None, None, None),
        P("row", "col", None),
    )
    return jax.shard_map(
        on_device,
        mesh=mesh,
        in_specs=placed,
        out_specs=P("row", "col", None, None, None),
        check_vma=False,
    )
```

```python
import functools

import jax
import jax.numpy as jnp
from jax import lax
from jax.experimental import pallas as pl
from jax.experimental.pallas import tpu as pltpu
from jax.sharding import PartitionSpec as P

STOPS = 4


def passed_along(value, axis, steps):
    count = lax.axis_size(axis)
    pairs = [(source, (source + steps) % count) for source in range(count)]
    return lax.ppermute(value, axis, pairs)


def bucketize(blocks, index):
    picked = jnp.take(blocks, jnp.maximum(index, 0), axis=0)
    return jnp.where((index >= 0)[..., None, None], picked, jnp.zeros_like(picked))


GROUP = 64


def stop_kernel(stop, first, last, stack_ref, map_ref, n_ref, send_ref, left_ref, right_ref, *refs):
    if first:
        acc_out_ref = refs[0]
        acc_ref = refs[-1] if last else acc_out_ref
    else:
        acc_in_ref, acc_out_ref = refs[0], refs[1]
        acc_ref = refs[-1] if last else acc_out_ref
    live_count = n_ref[stop]
    slots = map_ref.shape[1]
    left_count = left_ref.shape[0]
    right_count = right_ref.shape[0]
    result_count = acc_out_ref.shape[0]

    def per_group(g, carry):
        base = g * GROUP
        prods = []
        targets = []
        for k in range(GROUP):
            i = base + k
            slot = stack_ref[stop, 0, i]
            mapped = map_ref[stop, jnp.clip(slot, 0, slots - 1)]
            ok = (i < live_count) & (slot >= 0) & (mapped >= 0)
            a = left_ref[jnp.clip(mapped, 0, left_count - 1)]
            b = right_ref[jnp.clip(stack_ref[stop, 1, i], 0, right_count - 1)]
            p = jnp.dot(a, b, preferred_element_type=jnp.float32)
            p = p.astype(jnp.bfloat16).astype(jnp.float32)
            prods.append(jnp.where(ok, p, 0.0))
            targets.append(jnp.clip(stack_ref[stop, 2, i], 0, result_count - 1))
        for k in range(GROUP):
            t = targets[k]
            acc_ref[t] = acc_ref[t] + prods[k]
        return carry

    if first:
        acc_ref[...] = jnp.zeros(acc_ref.shape, jnp.float32)
    else:
        acc_ref[...] = acc_in_ref[...]
    lax.fori_loop(0, (live_count + GROUP - 1) // GROUP, per_group, 0)
    if last:
        for e in range(acc_out_ref.shape[0]):
            wanted = send_ref[e]
            block = acc_ref[jnp.clip(wanted, 0, result_count - 1)].astype(acc_out_ref.dtype)
            acc_out_ref[e] = jnp.where(wanted >= 0, block, jnp.zeros_like(block))


def run_stop(total, left, right, stacks, left_maps, live_counts, c_send, stop, last, result_shape):
    assert stacks.shape[-1] % GROUP == 0
    first = total is None
    full = lambda shape: pl.BlockSpec(shape, lambda *_: (0,) * len(shape))
    in_specs = [full(left.shape), full(right.shape)]
    operands = [stacks, left_maps, live_counts, c_send, left, right]
    aliases = {}
    if not first:
        in_specs.append(full(result_shape))
        operands.append(total)
        if not last:
            aliases = {6: 0}
    scratch = [pltpu.VMEM(result_shape, jnp.float32)] if last else []
    out_dtype = jnp.bfloat16 if last else jnp.float32
    out_shape = (c_send.shape[0],) + result_shape[1:] if last else result_shape
    grid_spec = pltpu.PrefetchScalarGridSpec(
        num_scalar_prefetch=4,
        grid=(1,),
        in_specs=in_specs,
        out_specs=full(out_shape),
        scratch_shapes=scratch,
    )
    return pl.pallas_call(
        functools.partial(stop_kernel, stop, first, last),
        grid_spec=grid_spec,
        out_shape=jax.ShapeDtypeStruct(out_shape, out_dtype),
        input_output_aliases=aliases,
    )(*operands)


def on_device(a_blocks, b_blocks, a_send, b_send, triples, c_send):
    rows_n = lax.axis_size("row")
    cols_n = lax.axis_size("col")
    count = rows_n * cols_n
    result_count = count // 2
    edge = a_blocks.shape[-1]
    left_out = bucketize(a_blocks[0, 0], a_send[0, 0])
    cap = left_out.shape[1]
    col_at = lax.axis_index("col")
    pieces = [jnp.take(left_out, col_at, axis=0)]
    for shift in range(1, cols_n):
        bucket = jnp.take(left_out, (col_at + shift) % cols_n, axis=0)
        pieces.append(passed_along(bucket, "col", shift))
    left_home = jnp.concatenate(pieces, axis=0)
    slot = jnp.arange(cols_n * cap, dtype=jnp.int32)[None, :]
    owner = (col_at + jnp.arange(STOPS, dtype=jnp.int32)[:, None]) % cols_n
    left_maps = (((owner - slot // cap) % cols_n) * cap + slot % cap).astype(jnp.int32)
    stacks = triples[0, 0].astype(jnp.int32)
    live_counts = jnp.sum((stacks[:, 0, :] >= 0).astype(jnp.int32), axis=1)
    right_out = bucketize(b_blocks[0, 0], b_send[0, 0])
    right_home = lax.all_to_all(right_out, "row", split_axis=0, concat_axis=0, tiled=True)
    right_home = right_home.reshape(-1, edge, edge)
    total = None
    result_shape = (result_count, edge, edge)
    left_now = left_home
    rights = [right_home] + [passed_along(right_home, "row", -s) for s in range(1, STOPS)]
    for stop_index in range(STOPS):
        right_now = rights[stop_index]
        if stop_index > 0:
            left_now = passed_along(left_now, "col", -1)
            left_now, total = lax.optimization_barrier((left_now, total))
        total = run_stop(total, left_now, right_now, stacks, left_maps, live_counts, c_send[0, 0], stop_index,
                         stop_index == STOPS - 1, result_shape)
    outgoing = total
    return lax.all_to_all(outgoing[None, None], ("row", "col"), split_axis=2, concat_axis=2, tiled=True)


def solution(mesh):
    placed = (
        P("row", "col", None, None, None),
        P("row", "col", None, None, None),
        P("row", "col", None, None),
        P("row", "col", None, None),
        P("row", "col", None, None, None),
        P("row", "col", None),
    )
    return jax.shard_map(
        on_device,
        mesh=mesh,
        in_specs=placed,
        out_specs=P("row", "col", None, None, None),
        check_vma=False,
    )
```

```python
import functools

import jax
import jax.numpy as jnp
from jax import lax
from jax.experimental import pallas as pl
from jax.experimental.pallas import tpu as pltpu
from jax.sharding import PartitionSpec as P

STOPS = 4


def passed_along(value, axis, steps):
    count = lax.axis_size(axis)
    pairs = [(source, (source + steps) % count) for source in range(count)]
    return lax.ppermute(value, axis, pairs)


def bucketize(blocks, index):
    picked = jnp.take(blocks, jnp.maximum(index, 0), axis=0)
    return jnp.where((index >= 0)[..., None, None], picked, jnp.zeros_like(picked))


GROUP = 96


def stop_kernel(stop, first, last, stack_ref, map_ref, n_ref, send_ref, left_ref, right_ref, *refs):
    if first:
        acc_out_ref = refs[0]
        acc_ref = refs[-1] if last else acc_out_ref
    else:
        acc_in_ref, acc_out_ref = refs[0], refs[1]
        acc_ref = refs[-1] if last else acc_out_ref
    live_count = n_ref[stop]
    slots = map_ref.shape[1]
    left_count = left_ref.shape[0]
    right_count = right_ref.shape[0]
    result_count = acc_out_ref.shape[0]

    def per_group(g, carry):
        base = g * GROUP
        prods = []
        targets = []
        for k in range(GROUP):
            i = base + k
            slot = stack_ref[stop, 0, i]
            mapped = map_ref[stop, jnp.clip(slot, 0, slots - 1)]
            ok = (i < live_count) & (slot >= 0) & (mapped >= 0)
            a = left_ref[jnp.clip(mapped, 0, left_count - 1)]
            b = right_ref[jnp.clip(stack_ref[stop, 1, i], 0, right_count - 1)]
            p = jnp.dot(a, b, preferred_element_type=jnp.float32)
            p = p.astype(jnp.bfloat16).astype(jnp.float32)
            prods.append(jnp.where(ok, p, 0.0))
            targets.append(jnp.clip(stack_ref[stop, 2, i], 0, result_count - 1))
        for k in range(GROUP):
            t = targets[k]
            acc_ref[t] = acc_ref[t] + prods[k]
        return carry

    if first:
        acc_ref[...] = jnp.zeros(acc_ref.shape, jnp.float32)
    else:
        acc_ref[...] = acc_in_ref[...]
    lax.fori_loop(0, (live_count + GROUP - 1) // GROUP, per_group, 0)
    if last:
        for e in range(acc_out_ref.shape[0]):
            wanted = send_ref[e]
            block = acc_ref[jnp.clip(wanted, 0, result_count - 1)].astype(acc_out_ref.dtype)
            acc_out_ref[e] = jnp.where(wanted >= 0, block, jnp.zeros_like(block))


def run_stop(total, left, right, stacks, left_maps, live_counts, c_send, stop, last, result_shape):
    assert stacks.shape[-1] % GROUP == 0
    first = total is None
    full = lambda shape: pl.BlockSpec(shape, lambda *_: (0,) * len(shape))
    in_specs = [full(left.shape), full(right.shape)]
    operands = [stacks, left_maps, live_counts, c_send, left, right]
    aliases = {}
    if not first:
        in_specs.append(full(result_shape))
        operands.append(total)
        if not last:
            aliases = {6: 0}
    scratch = [pltpu.VMEM(result_shape, jnp.float32)] if last else []
    out_dtype = jnp.bfloat16 if last else jnp.float32
    out_shape = (c_send.shape[0],) + result_shape[1:] if last else result_shape
    grid_spec = pltpu.PrefetchScalarGridSpec(
        num_scalar_prefetch=4,
        grid=(1,),
        in_specs=in_specs,
        out_specs=full(out_shape),
        scratch_shapes=scratch,
    )
    return pl.pallas_call(
        functools.partial(stop_kernel, stop, first, last),
        grid_spec=grid_spec,
        out_shape=jax.ShapeDtypeStruct(out_shape, out_dtype),
        input_output_aliases=aliases,
    )(*operands)


def on_device(a_blocks, b_blocks, a_send, b_send, triples, c_send):
    rows_n = lax.axis_size("row")
    cols_n = lax.axis_size("col")
    count = rows_n * cols_n
    result_count = count // 2
    edge = a_blocks.shape[-1]
    left_out = bucketize(a_blocks[0, 0], a_send[0, 0])
    cap = left_out.shape[1]
    col_at = lax.axis_index("col")
    pieces = [jnp.take(left_out, col_at, axis=0)]
    for shift in range(1, cols_n):
        bucket = jnp.take(left_out, (col_at + shift) % cols_n, axis=0)
        pieces.append(passed_along(bucket, "col", shift))
    left_home = jnp.concatenate(pieces, axis=0)
    slot = jnp.arange(cols_n * cap, dtype=jnp.int32)[None, :]
    owner = (col_at + jnp.arange(STOPS, dtype=jnp.int32)[:, None]) % cols_n
    left_maps = (((owner - slot // cap) % cols_n) * cap + slot % cap).astype(jnp.int32)
    stacks = triples[0, 0].astype(jnp.int32)
    live_counts = jnp.sum((stacks[:, 0, :] >= 0).astype(jnp.int32), axis=1)
    right_out = bucketize(b_blocks[0, 0], b_send[0, 0])
    right_home = lax.all_to_all(right_out, "row", split_axis=0, concat_axis=0, tiled=True)
    right_home = right_home.reshape(-1, edge, edge)
    total = None
    result_shape = (result_count, edge, edge)
    left_now = left_home
    rights = [right_home] + [passed_along(right_home, "row", -s) for s in range(1, STOPS)]
    for stop_index in range(STOPS):
        right_now = rights[stop_index]
        if stop_index > 0:
            left_now = passed_along(left_now, "col", -1)
            left_now, total = lax.optimization_barrier((left_now, total))
        total = run_stop(total, left_now, right_now, stacks, left_maps, live_counts, c_send[0, 0], stop_index,
                         stop_index == STOPS - 1, result_shape)
    outgoing = total
    return lax.all_to_all(outgoing[None, None], ("row", "col"), split_axis=2, concat_axis=2, tiled=True)


def solution(mesh):
    placed = (
        P("row", "col", None, None, None),
        P("row", "col", None, None, None),
        P("row", "col", None, None),
        P("row", "col", None, None),
        P("row", "col", None, None, None),
        P("row", "col", None),
    )
    return jax.shard_map(
        on_device,
        mesh=mesh,
        in_specs=placed,
        out_specs=P("row", "col", None, None, None),
        check_vma=False,
    )
```

```python
import functools

import jax
import jax.numpy as jnp
from jax import lax
from jax.experimental import pallas as pl
from jax.experimental.pallas import tpu as pltpu
from jax.sharding import PartitionSpec as P

STOPS = 4


def passed_along(value, axis, steps):
    count = lax.axis_size(axis)
    pairs = [(source, (source + steps) % count) for source in range(count)]
    return lax.ppermute(value, axis, pairs)


def bucketize(blocks, index):
    picked = jnp.take(blocks, jnp.maximum(index, 0), axis=0)
    return jnp.where((index >= 0)[..., None, None], picked, jnp.zeros_like(picked))


GROUP = 48


def stop_kernel(stop, first, last, stack_ref, map_ref, n_ref, send_ref, left_ref, right_ref, *refs):
    if first:
        acc_out_ref = refs[0]
        acc_ref = refs[-1] if last else acc_out_ref
    else:
        acc_in_ref, acc_out_ref = refs[0], refs[1]
        acc_ref = refs[-1] if last else acc_out_ref
    live_count = n_ref[stop]
    slots = map_ref.shape[1]
    left_count = left_ref.shape[0]
    right_count = right_ref.shape[0]
    result_count = acc_out_ref.shape[0]

    def per_group(g, carry):
        base = g * GROUP
        prods = []
        targets = []
        for k in range(GROUP):
            i = base + k
            slot = stack_ref[stop, 0, i]
            mapped = map_ref[stop, jnp.clip(slot, 0, slots - 1)]
            ok = (i < live_count) & (slot >= 0) & (mapped >= 0)
            a = left_ref[jnp.clip(mapped, 0, left_count - 1)]
            b = right_ref[jnp.clip(stack_ref[stop, 1, i], 0, right_count - 1)]
            p = jnp.dot(a, b, preferred_element_type=jnp.float32)
            p = p.astype(jnp.bfloat16).astype(jnp.float32)
            prods.append(jnp.where(ok, p, 0.0))
            targets.append(jnp.clip(stack_ref[stop, 2, i], 0, result_count - 1))
        for k in range(GROUP):
            t = targets[k]
            acc_ref[t] = acc_ref[t] + prods[k]
        return carry

    if first:
        acc_ref[...] = jnp.zeros(acc_ref.shape, jnp.float32)
    else:
        acc_ref[...] = acc_in_ref[...]
    lax.fori_loop(0, (live_count + GROUP - 1) // GROUP, per_group, 0)
    if last:
        for e in range(acc_out_ref.shape[0]):
            wanted = send_ref[e]
            block = acc_ref[jnp.clip(wanted, 0, result_count - 1)].astype(acc_out_ref.dtype)
            acc_out_ref[e] = jnp.where(wanted >= 0, block, jnp.zeros_like(block))


def run_stop(total, left, right, stacks, left_maps, live_counts, c_send, stop, last, result_shape):
    assert stacks.shape[-1] % GROUP == 0
    first = total is None
    full = lambda shape: pl.BlockSpec(shape, lambda *_: (0,) * len(shape))
    in_specs = [full(left.shape), full(right.shape)]
    operands = [stacks, left_maps, live_counts, c_send, left, right]
    aliases = {}
    if not first:
        in_specs.append(full(result_shape))
        operands.append(total)
        if not last:
            aliases = {6: 0}
    scratch = [pltpu.VMEM(result_shape, jnp.float32)] if last else []
    out_dtype = jnp.bfloat16 if last else jnp.float32
    out_shape = (c_send.shape[0],) + result_shape[1:] if last else result_shape
    grid_spec = pltpu.PrefetchScalarGridSpec(
        num_scalar_prefetch=4,
        grid=(1,),
        in_specs=in_specs,
        out_specs=full(out_shape),
        scratch_shapes=scratch,
    )
    return pl.pallas_call(
        functools.partial(stop_kernel, stop, first, last),
        grid_spec=grid_spec,
        out_shape=jax.ShapeDtypeStruct(out_shape, out_dtype),
        input_output_aliases=aliases,
    )(*operands)


def on_device(a_blocks, b_blocks, a_send, b_send, triples, c_send):
    rows_n = lax.axis_size("row")
    cols_n = lax.axis_size("col")
    count = rows_n * cols_n
    result_count = count // 2
    edge = a_blocks.shape[-1]
    left_out = bucketize(a_blocks[0, 0], a_send[0, 0])
    cap = left_out.shape[1]
    col_at = lax.axis_index("col")
    pieces = [jnp.take(left_out, col_at, axis=0)]
    for shift in range(1, cols_n):
        bucket = jnp.take(left_out, (col_at + shift) % cols_n, axis=0)
        pieces.append(passed_along(bucket, "col", shift))
    left_home = jnp.concatenate(pieces, axis=0)
    slot = jnp.arange(cols_n * cap, dtype=jnp.int32)[None, :]
    owner = (col_at + jnp.arange(STOPS, dtype=jnp.int32)[:, None]) % cols_n
    left_maps = (((owner - slot // cap) % cols_n) * cap + slot % cap).astype(jnp.int32)
    stacks = triples[0, 0].astype(jnp.int32)
    live_counts = jnp.sum((stacks[:, 0, :] >= 0).astype(jnp.int32), axis=1)
    right_out = bucketize(b_blocks[0, 0], b_send[0, 0])
    right_home = lax.all_to_all(right_out, "row", split_axis=0, concat_axis=0, tiled=True)
    right_home = right_home.reshape(-1, edge, edge)
    total = None
    result_shape = (result_count, edge, edge)
    left_now = left_home
    rights = [right_home] + [passed_along(right_home, "row", -s) for s in range(1, STOPS)]
    for stop_index in range(STOPS):
        right_now = rights[stop_index]
        if stop_index > 0:
            left_now = passed_along(left_now, "col", -1)
            left_now, total = lax.optimization_barrier((left_now, total))
        total = run_stop(total, left_now, right_now, stacks, left_maps, live_counts, c_send[0, 0], stop_index,
                         stop_index == STOPS - 1, result_shape)
    outgoing = total
    return lax.all_to_all(outgoing[None, None], ("row", "col"), split_axis=2, concat_axis=2, tiled=True)


def solution(mesh):
    placed = (
        P("row", "col", None, None, None),
        P("row", "col", None, None, None),
        P("row", "col", None, None),
        P("row", "col", None, None),
        P("row", "col", None, None, None),
        P("row", "col", None),
    )
    return jax.shard_map(
        on_device,
        mesh=mesh,
        in_specs=placed,
        out_specs=P("row", "col", None, None, None),
        check_vma=False,
    )
```
